128 devices in a mesh: ctx: 16 (over z, x_lo, core), head: 8 (over y, x_hi).
Axes of the slice: x: 4 (x_hi: 2, x_lo: 2; x = x_hi * 2 + x_lo), y: 4, z: 4, core: 2. Of those that a mesh axis runs over, the one named last changes fastest.
Arguments:
- queries: bfloat16 [24576, 3072], P('ctx', 'head'), may hold values from -160 to 160
- key_states: bfloat16 [24576, 3072], P('ctx', 'head'), may hold values from -12 to 12
- value_states: bfloat16 [24576, 3072], P('ctx', 'head'), may hold values from -18 to 18
- out_grads: bfloat16 [24576, 3072], P(('ctx', 'head')), may hold values from -6 to 6
- pattern: int32 [64, 8], replicated, may hold values from -1 to 63, as said below
Outputs:
- attended: bfloat16 [24576, 3072], P(('ctx', 'head'))
- query_grads: bfloat16 [24576, 3072], P('ctx', 'head')
- key_grads: bfloat16 [24576, 3072], P('ctx', 'head')
- value_grads: bfloat16 [24576, 3072], P('ctx', 'head')
The draws below stay inside these ranges and needn't reach their ends.
Inputs may be any that keep to these rules, and one draw needn't show every extreme that they name: `pattern`: row t lists distinct tiles whose frame tile (tile // 4) differs from that of t by at most one; t itself is always listed; -1 marks an empty slot and empty slots come last; three or more tiles are listed in every row.
All inputs are finite; a program needn't handle non-finite values.
Results may differ from the reference program's by a relative error of at most 0.035.
Values may be sent and summed in bfloat16 or wider, within the bound.
No kernel may reach another device: no remote copies, remote signals or barrier semaphores. Data moves between devices by JAX's collectives and lax.ppermute only.
A program may use at most 256 MiB of HBM per device.

```python
import math
import jax
import jax.numpy as jnp
from jax import lax

HEADS = 24
HD = 128
D = 3072
TILE = 384
SPT = 4
KSLOT = 8
TOKENS = 24576
TILES = 64


def shared_base(key):
    noise_q = jnp.clip(jax.random.normal(jax.random.fold_in(key, 11), (TOKENS, D), jnp.float32), -6.0, 6.0)
    noise_k = jnp.clip(jax.random.normal(jax.random.fold_in(key, 12), (TOKENS, D), jnp.float32), -6.0, 6.0)
    return (noise_q, noise_k)


def draw_queries(key, part):
    noise_q, noise_k = shared_base(key)
    result = noise_q
    return jnp.clip(result, -160.0, 160.0).astype(jnp.bfloat16)


def draw_key_states(key, part):
    noise_q, noise_k = shared_base(key)
    result = noise_k
    return jnp.clip(result, -12.0, 12.0).astype(jnp.bfloat16)


def draw_value_states(key, part):
    noise = jnp.clip(jax.random.normal(jax.random.fold_in(key, 21), (TOKENS, D), jnp.float32), -6.0, 6.0)
    return jnp.clip(noise, -18.0, 18.0).astype(jnp.bfloat16)


def draw_pattern(key, part):
    frame_tiles = TILES // SPT
    own_ids = jnp.arange(TILES, dtype=jnp.int32)
    frame_ids = own_ids // SPT
    offsets = jnp.arange(3 * SPT, dtype=jnp.int32)
    cand_frame = frame_ids[:, None] + offsets[None, :] // SPT - 1
    candidates = cand_frame * SPT + offsets[None, :] % SPT
    inside = (cand_frame >= 0) & (cand_frame < frame_tiles)
    ranking = jax.random.randint(jax.random.fold_in(key, 31), (TILES, 3 * SPT), 0, 1 << 20, jnp.int32) * (4 * SPT) + offsets[None, :]
    ranking = jnp.where(candidates == own_ids[:, None], -1, ranking)
    ranking = jnp.where(inside, ranking, 1 << 30)
    ordering = jnp.argsort(ranking, axis=1)
    picked = jnp.take_along_axis(candidates, ordering, axis=1)[:, :KSLOT]
    counts = jax.random.randint(jax.random.fold_in(key, 32), (TILES,), 3, KSLOT + 1, jnp.int32)
    counts = counts.at[0].set(KSLOT)
    slot_ids = jnp.arange(KSLOT, dtype=jnp.int32)
    return jnp.where(slot_ids[None, :] < counts[:, None], picked, -1).astype(jnp.int32)


def levels(key, shape, pieces, smallest, largest):
    level, own = 1.0, jax.random.fold_in(key, 6)
    for axis_at, parts in pieces:
        steps = jnp.exp(jax.random.uniform(jax.random.fold_in(own, axis_at), (parts,), jnp.float32, smallest / len(pieces), largest / len(pieces)))
        level = level * jnp.repeat(steps, shape[axis_at] // parts).reshape([-1 if axis == axis_at else 1 for axis in range(len(shape))])
    return level


def scatter_about(key, extent, scale, limit, shards=(), held_as=jnp.bfloat16):
    drawn = scale * jax.random.normal(key, extent, jnp.float32)
    if shards:
        drawn = drawn * levels(key, extent, shards, -0.22, 0.18)
    return jnp.clip(drawn, -limit, limit).astype(held_as)


def setup_inputs(seed: int = 0) -> dict:
    streams_of = jax.random.split(jax.random.key(seed), 6)
    return {
        "queries": draw_queries(jax.random.fold_in(streams_of[5], 71), 0),
        "key_states": draw_key_states(jax.random.fold_in(streams_of[5], 71), 0),
        "value_states": draw_value_states(jax.random.fold_in(streams_of[5], 71), 0),
        "out_grads": scatter_about(streams_of[3], (TOKENS, D), 1.0, 6.0, ((0, 128),)),
        "pattern": draw_pattern(jax.random.fold_in(streams_of[5], 71), 0),
    }


def slot_lookup(pattern, tile_num):
    listed = pattern[tile_num]
    allowed = listed >= 0
    safe_slots = jnp.where(allowed, listed, tile_num).astype(jnp.int32)
    return (allowed, safe_slots)

def tile_scores(query_tile, key_sel, allowed):
    score_scale = 1.0 / math.sqrt(HD)
    scores = jnp.einsum('qhd,sthd->hqst', query_tile.astype(jnp.float32), key_sel.astype(jnp.float32)) * score_scale
    return jnp.where(allowed[None, None, :, None], scores, -jnp.inf)

def reference(queries, key_states, value_states, out_grads, pattern):
    score_scale = 1.0 / math.sqrt(HD)
    query_tiles = queries.reshape(TILES, TILE, HEADS, HD)
    key_tiles = key_states.reshape(TILES, TILE, HEADS, HD)
    value_tiles = value_states.reshape(TILES, TILE, HEADS, HD)
    grad_tiles = out_grads.reshape(TILES, TILE, HEADS, HD)

    def forward_tile(tile_num):
        allowed, safe_slots = slot_lookup(pattern, tile_num)
        key_sel = key_tiles[safe_slots]
        value_sel = value_tiles[safe_slots]
        scores = tile_scores(query_tiles[tile_num], key_sel, allowed)
        row_max = lax.optimization_barrier(jnp.max(scores, axis=(2, 3)))
        row_total = lax.optimization_barrier(jnp.sum(jnp.exp(scores - row_max[:, :, None, None]), axis=(2, 3)))
        log_total = row_max + jnp.log(row_total)
        weights = jnp.exp(scores - log_total[:, :, None, None]).astype(jnp.bfloat16)
        result = jnp.einsum('hqst,sthd->qhd', weights.astype(jnp.float32), value_sel.astype(jnp.float32))
        return (result.astype(jnp.bfloat16), log_total)
    tile_ids = jnp.arange(TILES, dtype=jnp.int32)
    attended, log_totals = lax.map(forward_tile, tile_ids)
    delta = lax.optimization_barrier(jnp.sum(grad_tiles.astype(jnp.float32) * attended.astype(jnp.float32), axis=-1))

    def backward_tile(grad_sums, tile_num):
        allowed, safe_slots = slot_lookup(pattern, tile_num)
        key_sel = key_tiles[safe_slots]
        value_sel = value_tiles[safe_slots]
        query_tile = query_tiles[tile_num].astype(jnp.float32)
        grad_tile = grad_tiles[tile_num].astype(jnp.float32)
        scores = tile_scores(query_tiles[tile_num], key_sel, allowed)
        weights = jnp.exp(scores - log_totals[tile_num][:, :, None, None])
        weights_low = weights.astype(jnp.bfloat16)
        grad_weights = jnp.einsum('qhd,sthd->hqst', grad_tile, value_sel.astype(jnp.float32))
        delta_tile = jnp.transpose(delta[tile_num])
        grad_scores = (weights * (grad_weights - delta_tile[:, :, None, None])).astype(jnp.bfloat16)
        query_grad = jnp.einsum('hqst,sthd->qhd', grad_scores.astype(jnp.float32), key_sel.astype(jnp.float32)) * score_scale
        key_terms = jnp.einsum('hqst,qhd->sthd', grad_scores.astype(jnp.float32), query_tile) * score_scale
        value_terms = jnp.einsum('hqst,qhd->sthd', weights_low.astype(jnp.float32), grad_tile)
        keep = allowed[:, None, None, None]
        key_sums = grad_sums[0].at[safe_slots].add(jnp.where(keep, key_terms, 0.0))
        value_sums = grad_sums[1].at[safe_slots].add(jnp.where(keep, value_terms, 0.0))
        return ((key_sums, value_sums), query_grad.astype(jnp.bfloat16))
    zero_grads = jnp.zeros((TILES, TILE, HEADS, HD), jnp.float32)
    (key_sums, value_sums), query_grads = lax.scan(backward_tile, (zero_grads, zero_grads), tile_ids)
    return (attended.reshape(TOKENS, D), query_grads.reshape(TOKENS, D), key_sums.astype(jnp.bfloat16).reshape(TOKENS, D), value_sums.astype(jnp.bfloat16).reshape(TOKENS, D))
```

```python
import functools
import math

import jax
import jax.numpy as jnp
from jax import lax
from jax.experimental import pallas as pl
from jax.experimental.pallas import tpu as pltpu
from jax.sharding import PartitionSpec as P

HD = 128
TILE = 384
SPT = 4
KSLOT = 8
SCALE = 1.0 / math.sqrt(HD)
NT = (((1,), (1,)), ((), ()))
TN = (((0,), (0,)), ((), ()))


def with_halo(block, axis, dim):
    count = lax.axis_size(axis)
    forward = [(i, i + 1) for i in range(count - 1)]
    backward = [(target, source) for source, target in forward]
    low = lax.ppermute(block, axis, forward)
    high = lax.ppermute(block, axis, backward)
    return jnp.concatenate([low, block, high], axis=dim)


def from_behind(block, axis, distance):
    devices = range(lax.axis_size(axis))
    route = [(i - distance, i) for i in devices if i - distance in devices]
    return lax.ppermute(block, axis, route)


def attention_kernel(
    slots_ref, counts_ref, q_ref, do_ref, k_ref, v_ref,
    o_ref, dq_ref, dk_ref, dv_ref, s_scr,
):
    a = pl.program_id(1)

    @pl.when(a == 0)
    def _():
        dk_ref[...] = jnp.zeros_like(dk_ref)
        dv_ref[...] = jnp.zeros_like(dv_ref)

    q = q_ref[...]
    do = do_ref[...]
    count = counts_ref[a]

    def rows(s):
        start = pl.multiple_of(slots_ref[a * KSLOT + s] * TILE, TILE)
        return pl.ds(start, TILE)

    def score_pass(s, row_max):
        scores = lax.dot_general(
            q, k_ref[rows(s), :], NT, preferred_element_type=jnp.float32
        ) * SCALE
        s_scr[s] = scores
        return jnp.maximum(row_max, jnp.max(scores, axis=1, keepdims=True))

    row_max = lax.fori_loop(
        0, count, score_pass, jnp.full((TILE, 1), -jnp.inf, jnp.float32)
    )

    def exp_pass(s, row_total):
        e = jnp.exp(s_scr[s] - row_max)
        s_scr[s] = e
        return row_total + jnp.sum(e, axis=1, keepdims=True)

    row_total = lax.fori_loop(0, count, exp_pass, jnp.zeros((TILE, 1), jnp.float32))
    inv_total = 1.0 / row_total

    def value_pass(s, acc):
        w = (s_scr[s] * inv_total).astype(jnp.bfloat16)
        return acc + jnp.dot(w, v_ref[rows(s), :], preferred_element_type=jnp.float32)

    out = lax.fori_loop(0, count, value_pass, jnp.zeros((TILE, HD), jnp.float32))
    out = out.astype(jnp.bfloat16)
    o_ref[...] = out
    delta = jnp.sum(do.astype(jnp.float32) * out.astype(jnp.float32), axis=1, keepdims=True)

    def grad_pass(s, dq_acc):
        r = rows(s)
        w = s_scr[s] * inv_total
        g = lax.dot_general(do, v_ref[r, :], NT, preferred_element_type=jnp.float32)
        ds = (w * (g - delta)).astype(jnp.bfloat16)
        dk_ref[r, :] += lax.dot_general(ds, q, TN, preferred_element_type=jnp.float32)
        dv_ref[r, :] += lax.dot_general(
            w.astype(jnp.bfloat16), do, TN, preferred_element_type=jnp.float32
        )
        return dq_acc + jnp.dot(ds, k_ref[r, :], preferred_element_type=jnp.float32)

    dq = lax.fori_loop(0, count, grad_pass, jnp.zeros((TILE, HD), jnp.float32))
    dq_ref[...] = (dq * SCALE).astype(jnp.bfloat16)


def attention(slots, counts, queries, grads, keys, values):
    row_count, col_count = queries.shape
    heads = col_count // HD
    tiles = row_count // TILE
    ext_rows = keys.shape[0]
    tile_spec = pl.BlockSpec((TILE, HD), lambda h, a, sl, ct: (a, h))
    ext_spec = pl.BlockSpec((ext_rows, HD), lambda h, a, sl, ct: (0, h))
    return pl.pallas_call(
        attention_kernel,
        grid_spec=pltpu.PrefetchScalarGridSpec(
            num_scalar_prefetch=2,
            grid=(heads, tiles),
            in_specs=[tile_spec, tile_spec, ext_spec, ext_spec],
            out_specs=[tile_spec, tile_spec, ext_spec, ext_spec],
            scratch_shapes=[pltpu.VMEM((KSLOT, TILE, TILE), jnp.float32)],
        ),
        out_shape=[
            jax.ShapeDtypeStruct((row_count, col_count), jnp.bfloat16),
            jax.ShapeDtypeStruct((row_count, col_count), jnp.bfloat16),
            jax.ShapeDtypeStruct((ext_rows, col_count), jnp.float32),
            jax.ShapeDtypeStruct((ext_rows, col_count), jnp.float32),
        ],
        compiler_params=pltpu.CompilerParams(
            dimension_semantics=("arbitrary", "arbitrary"),
            vmem_limit_bytes=48 * 1024 * 1024,
        ),
    )(slots, counts, queries, grads, keys, values)


def shards(queries, key_states, value_states, out_grads, pattern):
    row_count, col_count = queries.shape
    own_tiles = row_count // TILE
    first_tile = lax.axis_index("ctx") * own_tiles
    base_tile = first_tile - SPT
    grads_heads = lax.all_to_all(out_grads, "head", split_axis=1, concat_axis=0, tiled=True)
    rims = with_halo(jnp.stack((key_states, value_states)), "ctx", 1)
    listed = lax.dynamic_slice_in_dim(pattern, first_tile, own_tiles, 0)
    allowed = listed >= 0
    slots = jnp.where(allowed, listed - base_tile, 0).reshape(-1).astype(jnp.int32)
    counts = jnp.sum(allowed.astype(jnp.int32), axis=1)
    out, dq, dk, dv = attention(slots, counts, queries, grads_heads, rims[0], rims[1])
    attended = lax.all_to_all(out, "head", split_axis=0, concat_axis=1, tiled=True)
    parts = jnp.stack((dk, dv))
    own_part = parts[:, row_count : 2 * row_count]
    lower_part = parts[:, :row_count].astype(jnp.bfloat16)
    upper_part = parts[:, 2 * row_count :].astype(jnp.bfloat16)
    from_above = from_behind(lower_part, "ctx", -1).astype(jnp.float32)
    from_below = from_behind(upper_part, "ctx", 1).astype(jnp.float32)
    total = own_part + from_above + from_below
    key_grads = (total[0] * SCALE).astype(jnp.bfloat16)
    value_grads = total[1].astype(jnp.bfloat16)
    return (attended, dq, key_grads, value_grads)


def solution(mesh):
    return jax.shard_map(
        shards,
        mesh=mesh,
        in_specs=(
            P("ctx", "head"),
            P("ctx", "head"),
            P("ctx", "head"),
            P(("ctx", "head"), None),
            P(),
        ),
        out_specs=(P(("ctx", "head"), None), P("ctx", "head"), P("ctx", "head"), P("ctx", "head")),
        check_vma=False,
    )
```

```python
import functools
import math

import jax
import jax.numpy as jnp
from jax import lax
from jax.experimental import pallas as pl
from jax.experimental.pallas import tpu as pltpu
from jax.sharding import PartitionSpec as P

HD = 128
TILE = 384
SPT = 4
KSLOT = 8
SCALE = 1.0 / math.sqrt(HD)
NT = (((1,), (1,)), ((), ()))
TN = (((0,), (0,)), ((), ()))


def with_halo(block, axis, dim):
    count = lax.axis_size(axis)
    forward = [(i, i + 1) for i in range(count - 1)]
    backward = [(target, source) for source, target in forward]
    low = lax.ppermute(block, axis, forward)
    high = lax.ppermute(block, axis, backward)
    return jnp.concatenate([low, block, high], axis=dim)


def from_behind(block, axis, distance):
    devices = range(lax.axis_size(axis))
    route = [(i - distance, i) for i in devices if i - distance in devices]
    return lax.ppermute(block, axis, route)


def attention_kernel(
    slots_ref, counts_ref, q_ref, do_ref, k_ref, v_ref,
    o_ref, dq_ref, dk_ref, dv_ref, s_scr,
):
    a = pl.program_id(0)

    @pl.when(a == 0)
    def _():
        dk_ref[...] = jnp.zeros_like(dk_ref)
        dv_ref[...] = jnp.zeros_like(dv_ref)

    q = q_ref[...]
    do = do_ref[...]
    count = counts_ref[a]

    def rows(s):
        start = pl.multiple_of(slots_ref[a * KSLOT + s] * TILE, TILE)
        return pl.ds(start, TILE)

    def score_pass(s, row_max):
        scores = lax.dot_general(
            q, k_ref[rows(s), :], NT, preferred_element_type=jnp.float32
        ) * SCALE
        s_scr[s] = scores
        return jnp.maximum(row_max, jnp.max(scores, axis=1, keepdims=True))

    row_max = lax.fori_loop(
        0, count, score_pass, jnp.full((TILE, 1), -jnp.inf, jnp.float32)
    )

    def exp_pass(s, row_total):
        e = jnp.exp(s_scr[s] - row_max)
        s_scr[s] = e
        return row_total + jnp.sum(e, axis=1, keepdims=True)

    row_total = lax.fori_loop(0, count, exp_pass, jnp.zeros((TILE, 1), jnp.float32))
    inv_total = 1.0 / row_total

    def value_pass(s, acc):
        w = (s_scr[s] * inv_total).astype(jnp.bfloat16)
        return acc + jnp.dot(w, v_ref[rows(s), :], preferred_element_type=jnp.float32)

    out = lax.fori_loop(0, count, value_pass, jnp.zeros((TILE, HD), jnp.float32))
    out = out.astype(jnp.bfloat16)
    o_ref[...] = out
    delta = jnp.sum(do.astype(jnp.float32) * out.astype(jnp.float32), axis=1, keepdims=True)

    def grad_pass(s, dq_acc):
        r = rows(s)
        w = s_scr[s] * inv_total
        g = lax.dot_general(do, v_ref[r, :], NT, preferred_element_type=jnp.float32)
        ds = (w * (g - delta)).astype(jnp.bfloat16)
        dk_ref[r, :] += lax.dot_general(ds, q, TN, preferred_element_type=jnp.float32)
        dv_ref[r, :] += lax.dot_general(
            w.astype(jnp.bfloat16), do, TN, preferred_element_type=jnp.float32
        )
        return dq_acc + jnp.dot(ds, k_ref[r, :], preferred_element_type=jnp.float32)

    dq = lax.fori_loop(0, count, grad_pass, jnp.zeros((TILE, HD), jnp.float32))
    dq_ref[...] = (dq * SCALE).astype(jnp.bfloat16)


def attention(slots, counts, queries, grads, keys, values, head):
    row_count = queries.shape[0]
    tiles = row_count // TILE
    ext_rows = keys.shape[0]
    in_spec = pl.BlockSpec((TILE, HD), lambda a, sl, ct: (a, head))
    tile_spec = pl.BlockSpec((TILE, HD), lambda a, sl, ct: (a, 0))
    ext_spec = pl.BlockSpec((ext_rows, HD), lambda a, sl, ct: (0, 0))
    return pl.pallas_call(
        attention_kernel,
        grid_spec=pltpu.PrefetchScalarGridSpec(
            num_scalar_prefetch=2,
            grid=(tiles,),
            in_specs=[in_spec, in_spec, ext_spec, ext_spec],
            out_specs=[tile_spec, tile_spec, ext_spec, ext_spec],
            scratch_shapes=[pltpu.VMEM((KSLOT, TILE, TILE), jnp.float32)],
        ),
        out_shape=[
            jax.ShapeDtypeStruct((row_count, HD), jnp.bfloat16),
            jax.ShapeDtypeStruct((row_count, HD), jnp.bfloat16),
            jax.ShapeDtypeStruct((ext_rows, HD), jnp.float32),
            jax.ShapeDtypeStruct((ext_rows, HD), jnp.float32),
        ],
        compiler_params=pltpu.CompilerParams(
            dimension_semantics=("arbitrary",),
            vmem_limit_bytes=48 * 1024 * 1024,
        ),
    )(slots, counts, queries, grads, keys, values)


def shards(queries, key_states, value_states, out_grads, pattern):
    row_count, col_count = queries.shape
    heads = col_count // HD
    own_tiles = row_count // TILE
    first_tile = lax.axis_index("ctx") * own_tiles
    base_tile = first_tile - SPT
    grads_heads = lax.all_to_all(out_grads, "head", split_axis=1, concat_axis=0, tiled=True)
    listed = lax.dynamic_slice_in_dim(pattern, first_tile, own_tiles, 0)
    allowed = listed >= 0
    slots = jnp.where(allowed, listed - base_tile, 0).reshape(-1).astype(jnp.int32)
    counts = jnp.sum(allowed.astype(jnp.int32), axis=1)
    outs, dqs, dks, dvs = [], [], [], []
    first = jnp.stack((key_states[:, :HD], value_states[:, :HD]))
    rest = jnp.stack((key_states[:, HD:], value_states[:, HD:]))
    halos = [with_halo(first, "ctx", 1), with_halo(rest, "ctx", 1)]
    for h in range(heads):
        cols = slice(h * HD, (h + 1) * HD)
        rims = halos[0] if h == 0 else halos[1][:, :, (h - 1) * HD : h * HD]
        with jax.named_scope(f"attention_head{h}"):
            out, dq, dk, dv = attention(
                slots, counts, queries, grads_heads, rims[0], rims[1], h
            )
        parts = jnp.stack((dk, dv))
        own_part = parts[:, row_count : 2 * row_count]
        lower_part = parts[:, :row_count].astype(jnp.bfloat16)
        upper_part = parts[:, 2 * row_count :].astype(jnp.bfloat16)
        from_above = from_behind(lower_part, "ctx", -1).astype(jnp.float32)
        from_below = from_behind(upper_part, "ctx", 1).astype(jnp.float32)
        total = own_part + from_above + from_below
        outs.append(out)
        dqs.append(dq)
        dks.append((total[0] * SCALE).astype(jnp.bfloat16))
        dvs.append(total[1].astype(jnp.bfloat16))
    out = jnp.concatenate(outs, axis=1)
    attended = lax.all_to_all(out, "head", split_axis=0, concat_axis=1, tiled=True)
    cat = functools.partial(jnp.concatenate, axis=1)
    return (attended, cat(dqs), cat(dks), cat(dvs))


def solution(mesh):
    return jax.shard_map(
        shards,
        mesh=mesh,
        in_specs=(
            P("ctx", "head"),
            P("ctx", "head"),
            P("ctx", "head"),
            P(("ctx", "head"), None),
            P(),
        ),
        out_specs=(P(("ctx", "head"), None), P("ctx", "head"), P("ctx", "head"), P("ctx", "head")),
        check_vma=False,
    )
```

```python
import functools
import math

import jax
import jax.numpy as jnp
from jax import lax
from jax.experimental import pallas as pl
from jax.experimental.pallas import tpu as pltpu
from jax.sharding import PartitionSpec as P

HD = 128
TILE = 384
SPT = 4
KSLOT = 8
SCALE = 1.0 / math.sqrt(HD)
NT = (((1,), (1,)), ((), ()))
TN = (((0,), (0,)), ((), ()))


def with_halo(block, axis, dim):
    count = lax.axis_size(axis)
    forward = [(i, i + 1) for i in range(count - 1)]
    backward = [(target, source) for source, target in forward]
    low = lax.ppermute(block, axis, forward)
    high = lax.ppermute(block, axis, backward)
    return jnp.concatenate([low, block, high], axis=dim)


def from_behind(block, axis, distance):
    devices = range(lax.axis_size(axis))
    route = [(i - distance, i) for i in devices if i - distance in devices]
    return lax.ppermute(block, axis, route)


def attention_kernel(
    slots_ref, counts_ref, q_ref, do_ref, k_ref, v_ref,
    o_ref, dq_ref, dk_ref, dv_ref, s_scr,
):
    a = pl.program_id(0)

    @pl.when(a == 0)
    def _():
        dk_ref[...] = jnp.zeros_like(dk_ref)
        dv_ref[...] = jnp.zeros_like(dv_ref)

    q = q_ref[...]
    do = do_ref[...]
    count = counts_ref[a]

    def rows(s):
        start = pl.multiple_of(slots_ref[a * KSLOT + s] * TILE, TILE)
        return pl.ds(start, TILE)

    def score_pass(s, row_max):
        scores = lax.dot_general(
            q, k_ref[rows(s), :], NT, preferred_element_type=jnp.float32
        ) * SCALE
        s_scr[s] = scores
        return jnp.maximum(row_max, jnp.max(scores, axis=1, keepdims=True))

    row_max = lax.fori_loop(
        0, count, score_pass, jnp.full((TILE, 1), -jnp.inf, jnp.float32)
    )

    def exp_pass(s, row_total):
        e = jnp.exp(s_scr[s] - row_max)
        s_scr[s] = e
        return row_total + jnp.sum(e, axis=1, keepdims=True)

    row_total = lax.fori_loop(0, count, exp_pass, jnp.zeros((TILE, 1), jnp.float32))
    inv_total = 1.0 / row_total

    def value_pass(s, acc):
        w = (s_scr[s] * inv_total).astype(jnp.bfloat16)
        return acc + jnp.dot(w, v_ref[rows(s), :], preferred_element_type=jnp.float32)

    out = lax.fori_loop(0, count, value_pass, jnp.zeros((TILE, HD), jnp.float32))
    out = out.astype(jnp.bfloat16)
    o_ref[...] = out
    delta = jnp.sum(do.astype(jnp.float32) * out.astype(jnp.float32), axis=1, keepdims=True)

    def grad_pass(s, dq_acc):
        r = rows(s)
        w = s_scr[s] * inv_total
        g = lax.dot_general(do, v_ref[r, :], NT, preferred_element_type=jnp.float32)
        ds = (w * (g - delta)).astype(jnp.bfloat16)
        dk_ref[r, :] += lax.dot_general(ds, q, TN, preferred_element_type=jnp.float32)
        dv_ref[r, :] += lax.dot_general(
            w.astype(jnp.bfloat16), do, TN, preferred_element_type=jnp.float32
        )
        return dq_acc + jnp.dot(ds, k_ref[r, :], preferred_element_type=jnp.float32)

    dq = lax.fori_loop(0, count, grad_pass, jnp.zeros((TILE, HD), jnp.float32))
    dq_ref[...] = (dq * SCALE).astype(jnp.bfloat16)


def attention(slots, counts, queries, grads, keys, values, head):
    row_count = queries.shape[0]
    tiles = row_count // TILE
    ext_rows = keys.shape[0]
    in_spec = pl.BlockSpec((TILE, HD), lambda a, sl, ct: (a, head))
    grad_spec = pl.BlockSpec((TILE, HD), lambda a, sl, ct: (a, 0))
    tile_spec = pl.BlockSpec((TILE, HD), lambda a, sl, ct: (a, 0))
    ext_spec = pl.BlockSpec((ext_rows, HD), lambda a, sl, ct: (0, 0))
    return pl.pallas_call(
        attention_kernel,
        grid_spec=pltpu.PrefetchScalarGridSpec(
            num_scalar_prefetch=2,
            grid=(tiles,),
            in_specs=[in_spec, grad_spec, ext_spec, ext_spec],
            out_specs=[tile_spec, tile_spec, ext_spec, ext_spec],
            scratch_shapes=[pltpu.VMEM((KSLOT, TILE, TILE), jnp.float32)],
        ),
        out_shape=[
            jax.ShapeDtypeStruct((row_count, HD), jnp.bfloat16),
            jax.ShapeDtypeStruct((row_count, HD), jnp.bfloat16),
            jax.ShapeDtypeStruct((ext_rows, HD), jnp.float32),
            jax.ShapeDtypeStruct((ext_rows, HD), jnp.float32),
        ],
        compiler_params=pltpu.CompilerParams(
            dimension_semantics=("arbitrary",),
            vmem_limit_bytes=48 * 1024 * 1024,
        ),
    )(slots, counts, queries, grads, keys, values)


def shards(queries, key_states, value_states, out_grads, pattern):
    row_count, col_count = queries.shape
    heads = col_count // HD
    own_tiles = row_count // TILE
    first_tile = lax.axis_index("ctx") * own_tiles
    base_tile = first_tile - SPT
    groups = lax.axis_size("head")
    token_rows = out_grads.shape[0]
    grads_split = out_grads.reshape(token_rows, groups, heads, HD)
    grads_heads = [
        lax.all_to_all(
            grads_split[:, :, h].reshape(token_rows, groups * HD),
            "head", split_axis=1, concat_axis=0, tiled=True,
        )
        for h in range(heads)
    ]
    listed = lax.dynamic_slice_in_dim(pattern, first_tile, own_tiles, 0)
    allowed = listed >= 0
    slots = jnp.where(allowed, listed - base_tile, 0).reshape(-1).astype(jnp.int32)
    counts = jnp.sum(allowed.astype(jnp.int32), axis=1)
    outs, dqs, dks, dvs = [], [], [], []
    first = jnp.stack((key_states[:, :HD], value_states[:, :HD]))
    rest = jnp.stack((key_states[:, HD:], value_states[:, HD:]))
    halos = [with_halo(first, "ctx", 1), with_halo(rest, "ctx", 1)]
    for h in range(heads):
        cols = slice(h * HD, (h + 1) * HD)
        rims = halos[0] if h == 0 else halos[1][:, :, (h - 1) * HD : h * HD]
        with jax.named_scope(f"attention_head{h}"):
            out, dq, dk, dv = attention(
                slots, counts, queries, grads_heads[h], rims[0], rims[1], h
            )
        parts = jnp.stack((dk, dv))
        own_part = parts[:, row_count : 2 * row_count]
        lower_part = parts[:, :row_count].astype(jnp.bfloat16)
        upper_part = parts[:, 2 * row_count :].astype(jnp.bfloat16)
        from_above = from_behind(lower_part, "ctx", -1).astype(jnp.float32)
        from_below = from_behind(upper_part, "ctx", 1).astype(jnp.float32)
        total = own_part + from_above + from_below
        outs.append(lax.all_to_all(out, "head", split_axis=0, concat_axis=1, tiled=True))
        dqs.append(dq)
        dks.append((total[0] * SCALE).astype(jnp.bfloat16))
        dvs.append(total[1].astype(jnp.bfloat16))
    attended = jnp.stack(
        [o.reshape(token_rows, groups, HD) for o in outs], axis=2
    ).reshape(token_rows, groups * heads * HD)
    cat = functools.partial(jnp.concatenate, axis=1)
    return (attended, cat(dqs), cat(dks), cat(dvs))


def solution(mesh):
    return jax.shard_map(
        shards,
        mesh=mesh,
        in_specs=(
            P("ctx", "head"),
            P("ctx", "head"),
            P("ctx", "head"),
            P(("ctx", "head"), None),
            P(),
        ),
        out_specs=(P(("ctx", "head"), None), P("ctx", "head"), P("ctx", "head"), P("ctx", "head")),
        check_vma=False,
    )
```

```python
import functools
import math

import jax
import jax.numpy as jnp
from jax import lax
from jax.experimental import pallas as pl
from jax.experimental.pallas import tpu as pltpu
from jax.sharding import PartitionSpec as P

HD = 128
TILE = 384
SPT = 4
KSLOT = 8
SCALE = 1.0 / math.sqrt(HD)
NT = (((1,), (1,)), ((), ()))
TN = (((0,), (0,)), ((), ()))


def with_halo(block, axis, dim):
    count = lax.axis_size(axis)
    forward = [(i, i + 1) for i in range(count - 1)]
    backward = [(target, source) for source, target in forward]
    low = lax.ppermute(block, axis, forward)
    high = lax.ppermute(block, axis, backward)
    return jnp.concatenate([low, block, high], axis=dim)


def from_behind(block, axis, distance):
    devices = range(lax.axis_size(axis))
    route = [(i - distance, i) for i in devices if i - distance in devices]
    return lax.ppermute(block, axis, route)


def attention_kernel(
    slots_ref, counts_ref, q_ref, do_ref, qt_ref, dot_ref, k_ref, v_ref,
    o_ref, dq_ref, dk_ref, dv_ref, s_scr,
):
    a = pl.program_id(1)

    @pl.when(a == 0)
    def _():
        dk_ref[...] = jnp.zeros_like(dk_ref)
        dv_ref[...] = jnp.zeros_like(dv_ref)

    q = q_ref[...]
    do = do_ref[...]
    count = counts_ref[a]

    def rows(s):
        start = pl.multiple_of(slots_ref[a * KSLOT + s] * TILE, TILE)
        return pl.ds(start, TILE)

    def lane_fold(x, op):
        parts = [x[:, j * HD : (j + 1) * HD] for j in range(TILE // HD)]
        return functools.reduce(op, parts)

    def score_pass(s, row_max):
        scores = lax.dot_general(
            q, k_ref[rows(s), :], NT, preferred_element_type=jnp.float32
        ) * SCALE
        s_scr[s] = scores
        return jnp.maximum(row_max, lane_fold(scores, jnp.maximum))

    row_max = lax.fori_loop(
        0, count, score_pass, jnp.full((TILE, HD), -jnp.inf, jnp.float32)
    )
    row_max = jnp.max(row_max, axis=1, keepdims=True)

    def exp_pass(s, carry):
        row_total, acc = carry
        e = jnp.exp(s_scr[s] - row_max)
        s_scr[s] = e
        acc = acc + jnp.dot(
            e.astype(jnp.bfloat16), v_ref[rows(s), :], preferred_element_type=jnp.float32
        )
        return row_total + lane_fold(e, jnp.add), acc

    row_total, acc = lax.fori_loop(
        0, count, exp_pass,
        (jnp.zeros((TILE, HD), jnp.float32), jnp.zeros((TILE, HD), jnp.float32)),
    )
    inv_total = 1.0 / jnp.sum(row_total, axis=1, keepdims=True)
    out = (acc * inv_total).astype(jnp.bfloat16)
    o_ref[...] = out
    delta = jnp.sum(do.astype(jnp.float32) * out.astype(jnp.float32), axis=1, keepdims=True)

    def grad_pass(s, dq_acc):
        r = rows(s)
        w = s_scr[s] * inv_total
        g = lax.dot_general(do, v_ref[r, :], NT, preferred_element_type=jnp.float32)
        ds = (w * (g - delta)).astype(jnp.bfloat16)
        slot = slots_ref[a * KSLOT + s]
        dk_ref[slot] += jnp.dot(qt_ref[0], ds, preferred_element_type=jnp.float32)
        dv_ref[slot] += jnp.dot(
            dot_ref[0], w.astype(jnp.bfloat16), preferred_element_type=jnp.float32
        )
        return dq_acc + jnp.dot(ds, k_ref[r, :], preferred_element_type=jnp.float32)

    dq = lax.fori_loop(0, count, grad_pass, jnp.zeros((TILE, HD), jnp.float32))
    dq_ref[...] = (dq * SCALE).astype(jnp.bfloat16)


def attention(slots, counts, queries, grads, keys, values):
    row_count, col_count = queries.shape
    heads = col_count // HD
    tiles = row_count // TILE
    ext_rows = keys.shape[0]
    ext_tiles = ext_rows // TILE
    queries_t = queries.reshape(tiles, TILE, col_count).transpose(0, 2, 1)
    grads_t = grads.reshape(tiles, TILE, col_count).transpose(0, 2, 1)
    tile_spec = pl.BlockSpec((TILE, HD), lambda h, a, sl, ct: (a, h))
    t_spec = pl.BlockSpec((1, HD, TILE), lambda h, a, sl, ct: (a, h, 0))
    ext_spec = pl.BlockSpec((ext_rows, HD), lambda h, a, sl, ct: (0, h))
    acc_spec = pl.BlockSpec((ext_tiles, HD, TILE), lambda h, a, sl, ct: (0, h, 0))
    return pl.pallas_call(
        attention_kernel,
        grid_spec=pltpu.PrefetchScalarGridSpec(
            num_scalar_prefetch=2,
            grid=(heads, tiles),
            in_specs=[tile_spec, tile_spec, t_spec, t_spec, ext_spec, ext_spec],
            out_specs=[tile_spec, tile_spec, acc_spec, acc_spec],
            scratch_shapes=[pltpu.VMEM((KSLOT, TILE, TILE), jnp.float32)],
        ),
        out_shape=[
            jax.ShapeDtypeStruct((row_count, col_count), jnp.bfloat16),
            jax.ShapeDtypeStruct((row_count, col_count), jnp.bfloat16),
            jax.ShapeDtypeStruct((ext_tiles, col_count, TILE), jnp.float32),
            jax.ShapeDtypeStruct((ext_tiles, col_count, TILE), jnp.float32),
        ],
        compiler_params=pltpu.CompilerParams(
            dimension_semantics=("arbitrary", "arbitrary"),
            vmem_limit_bytes=48 * 1024 * 1024,
        ),
    )(slots, counts, queries, grads, queries_t, grads_t, keys, values)


def shards(queries, key_states, value_states, out_grads, pattern):
    row_count, col_count = queries.shape
    own_tiles = row_count // TILE
    first_tile = lax.axis_index("ctx") * own_tiles
    base_tile = first_tile - SPT
    grads_heads = lax.all_to_all(out_grads, "head", split_axis=1, concat_axis=0, tiled=True)
    rims = with_halo(jnp.stack((key_states, value_states)), "ctx", 1)
    listed = lax.dynamic_slice_in_dim(pattern, first_tile, own_tiles, 0)
    allowed = listed >= 0
    slots = jnp.where(allowed, listed - base_tile, 0).reshape(-1).astype(jnp.int32)
    counts = jnp.sum(allowed.astype(jnp.int32), axis=1)
    out, dq, dk, dv = attention(slots, counts, queries, grads_heads, rims[0], rims[1])
    attended = lax.all_to_all(out, "head", split_axis=0, concat_axis=1, tiled=True)
    parts = jnp.stack((dk, dv)).transpose(0, 1, 3, 2).reshape(2, -1, col_count)
    own_part = parts[:, row_count : 2 * row_count]
    lower_part = parts[:, :row_count].astype(jnp.bfloat16)
    upper_part = parts[:, 2 * row_count :].astype(jnp.bfloat16)
    from_above = from_behind(lower_part, "ctx", -1).astype(jnp.float32)
    from_below = from_behind(upper_part, "ctx", 1).astype(jnp.float32)
    total = own_part + from_above + from_below
    key_grads = (total[0] * SCALE).astype(jnp.bfloat16)
    value_grads = total[1].astype(jnp.bfloat16)
    return (attended, dq, key_grads, value_grads)


def solution(mesh):
    return jax.shard_map(
        shards,
        mesh=mesh,
        in_specs=(
            P("ctx", "head"),
            P("ctx", "head"),
            P("ctx", "head"),
            P(("ctx", "head"), None),
            P(),
        ),
        out_specs=(P(("ctx", "head"), None), P("ctx", "head"), P("ctx", "head"), P("ctx", "head")),
        check_vma=False,
    )
```

```python
import functools
import math

import jax
import jax.numpy as jnp
from jax import lax
from jax.experimental import pallas as pl
from jax.experimental.pallas import tpu as pltpu
from jax.sharding import PartitionSpec as P

HD = 128
TILE = 384
SPT = 4
KSLOT = 8
SCALE = 1.0 / math.sqrt(HD)
NT = (((1,), (1,)), ((), ()))
TN = (((0,), (0,)), ((), ()))


def with_halo(block, axis, dim):
    count = lax.axis_size(axis)
    forward = [(i, i + 1) for i in range(count - 1)]
    backward = [(target, source) for source, target in forward]
    low = lax.ppermute(block, axis, forward)
    high = lax.ppermute(block, axis, backward)
    return jnp.concatenate([low, block, high], axis=dim)


def from_behind(block, axis, distance):
    devices = range(lax.axis_size(axis))
    route = [(i - distance, i) for i in devices if i - distance in devices]
    return lax.ppermute(block, axis, route)


def lane_fold(x, op):
    parts = [x[:, j * HD : (j + 1) * HD] for j in range(x.shape[1] // HD)]
    return functools.reduce(op, parts)


def slot_rows(slots_ref, a, s):
    start = pl.multiple_of(slots_ref[a * KSLOT + s] * TILE, TILE)
    return pl.ds(start, TILE)


def forward_kernel(slots_ref, counts_ref, q_ref, k_ref, v_ref, o_ref, lse_ref, s_scr):
    a = pl.program_id(1)
    q = q_ref[...]
    count = counts_ref[a]
    rows = functools.partial(slot_rows, slots_ref, a)

    def score_pass(s, row_max):
        scores = lax.dot_general(
            q, k_ref[rows(s), :], NT, preferred_element_type=jnp.float32
        ) * SCALE
        s_scr[s] = scores
        return jnp.maximum(row_max, lane_fold(scores, jnp.maximum))

    row_max = lax.fori_loop(
        0, count, score_pass, jnp.full((TILE, HD), -jnp.inf, jnp.float32)
    )
    row_max = jnp.max(row_max, axis=1, keepdims=True)

    def exp_pass(s, carry):
        row_total, acc = carry
        e = jnp.exp(s_scr[s] - row_max)
        acc = acc + jnp.dot(
            e.astype(jnp.bfloat16), v_ref[rows(s), :], preferred_element_type=jnp.float32
        )
        return row_total + lane_fold(e, jnp.add), acc

    row_total, acc = lax.fori_loop(
        0, count, exp_pass,
        (jnp.zeros((TILE, HD), jnp.float32), jnp.zeros((TILE, HD), jnp.float32)),
    )
    row_total = jnp.sum(row_total, axis=1, keepdims=True)
    o_ref[...] = (acc * (1.0 / row_total)).astype(jnp.bfloat16)
    lse_ref[...] = jnp.broadcast_to(row_max + jnp.log(row_total), (TILE, HD))


def backward_kernel(
    slots_ref, counts_ref, q_ref, do_ref, o_ref, lse_ref, k_ref, v_ref,
    dq_ref, dk_ref, dv_ref,
):
    a = pl.program_id(1)

    @pl.when(a == 0)
    def _():
        dk_ref[...] = jnp.zeros_like(dk_ref)
        dv_ref[...] = jnp.zeros_like(dv_ref)

    q = q_ref[...]
    do = do_ref[...]
    lse = lse_ref[:, :1]
    delta = jnp.sum(
        do.astype(jnp.float32) * o_ref[...].astype(jnp.float32), axis=1, keepdims=True
    )
    count = counts_ref[a]
    rows = functools.partial(slot_rows, slots_ref, a)

    def grad_pass(s, dq_acc):
        r = rows(s)
        k = k_ref[r, :]
        scores = lax.dot_general(q, k, NT, preferred_element_type=jnp.float32) * SCALE
        w = jnp.exp(scores - lse)
        g = lax.dot_general(do, v_ref[r, :], NT, preferred_element_type=jnp.float32)
        ds = (w * (g - delta)).astype(jnp.bfloat16)
        dk_ref[r, :] += lax.dot_general(ds, q, TN, preferred_element_type=jnp.float32)
        dv_ref[r, :] += lax.dot_general(
            w.astype(jnp.bfloat16), do, TN, preferred_element_type=jnp.float32
        )
        return dq_acc + jnp.dot(ds, k, preferred_element_type=jnp.float32)

    dq = lax.fori_loop(0, count, grad_pass, jnp.zeros((TILE, HD), jnp.float32))
    dq_ref[...] = (dq * SCALE).astype(jnp.bfloat16)


def specs(row_count, ext_rows):
    tile_spec = pl.BlockSpec((TILE, HD), lambda h, a, sl, ct: (a, h))
    ext_spec = pl.BlockSpec((ext_rows, HD), lambda h, a, sl, ct: (0, h))
    return tile_spec, ext_spec


def attention_forward(slots, counts, queries, keys, values):
    row_count, col_count = queries.shape
    tile_spec, ext_spec = specs(row_count, keys.shape[0])
    return pl.pallas_call(
        forward_kernel,
        grid_spec=pltpu.PrefetchScalarGridSpec(
            num_scalar_prefetch=2,
            grid=(col_count // HD, row_count // TILE),
            in_specs=[tile_spec, ext_spec, ext_spec],
            out_specs=[tile_spec, tile_spec],
            scratch_shapes=[pltpu.VMEM((KSLOT, TILE, TILE), jnp.float32)],
        ),
        out_shape=[
            jax.ShapeDtypeStruct((row_count, col_count), jnp.bfloat16),
            jax.ShapeDtypeStruct((row_count, col_count), jnp.float32),
        ],
        compiler_params=pltpu.CompilerParams(
            dimension_semantics=("arbitrary", "arbitrary"),
            vmem_limit_bytes=48 * 1024 * 1024,
        ),
    )(slots, counts, queries, keys, values)


def attention_backward(slots, counts, queries, grads, out, lse, keys, values):
    row_count, col_count = queries.shape
    ext_rows = keys.shape[0]
    tile_spec, ext_spec = specs(row_count, ext_rows)
    return pl.pallas_call(
        backward_kernel,
        grid_spec=pltpu.PrefetchScalarGridSpec(
            num_scalar_prefetch=2,
            grid=(col_count // HD, row_count // TILE),
            in_specs=[tile_spec, tile_spec, tile_spec, tile_spec, ext_spec, ext_spec],
            out_specs=[tile_spec, ext_spec, ext_spec],
        ),
        out_shape=[
            jax.ShapeDtypeStruct((row_count, col_count), jnp.bfloat16),
            jax.ShapeDtypeStruct((ext_rows, col_count), jnp.float32),
            jax.ShapeDtypeStruct((ext_rows, col_count), jnp.float32),
        ],
        compiler_params=pltpu.CompilerParams(
            dimension_semantics=("arbitrary", "arbitrary"),
            vmem_limit_bytes=48 * 1024 * 1024,
        ),
    )(slots, counts, queries, grads, out, lse, keys, values)


def shards(queries, key_states, value_states, out_grads, pattern):
    row_count, col_count = queries.shape
    own_tiles = row_count // TILE
    first_tile = lax.axis_index("ctx") * own_tiles
    base_tile = first_tile - SPT
    rims = with_halo(jnp.stack((key_states, value_states)), "ctx", 1)
    grads_heads = lax.all_to_all(out_grads, "head", split_axis=1, concat_axis=0, tiled=True)
    listed = lax.dynamic_slice_in_dim(pattern, first_tile, own_tiles, 0)
    allowed = listed >= 0
    slots = jnp.where(allowed, listed - base_tile, 0).reshape(-1).astype(jnp.int32)
    counts = jnp.sum(allowed.astype(jnp.int32), axis=1)
    out, lse = attention_forward(slots, counts, queries, rims[0], rims[1])
    attended = lax.all_to_all(out, "head", split_axis=0, concat_axis=1, tiled=True)
    dq, dk, dv = attention_backward(
        slots, counts, queries, grads_heads, out, lse, rims[0], rims[1]
    )
    parts = jnp.stack((dk, dv))
    own_part = parts[:, row_count : 2 * row_count]
    lower_part = parts[:, :row_count].astype(jnp.bfloat16)
    upper_part = parts[:, 2 * row_count :].astype(jnp.bfloat16)
    from_above = from_behind(lower_part, "ctx", -1).astype(jnp.float32)
    from_below = from_behind(upper_part, "ctx", 1).astype(jnp.float32)
    total = own_part + from_above + from_below
    key_grads = (total[0] * SCALE).astype(jnp.bfloat16)
    value_grads = total[1].astype(jnp.bfloat16)
    return (attended, dq, key_grads, value_grads)


def solution(mesh):
    return jax.shard_map(
        shards,
        mesh=mesh,
        in_specs=(
            P("ctx", "head"),
            P("ctx", "head"),
            P("ctx", "head"),
            P(("ctx", "head"), None),
            P(),
        ),
        out_specs=(P(("ctx", "head"), None), P("ctx", "head"), P("ctx", "head"), P("ctx", "head")),
        check_vma=False,
    )
```

```python
import functools
import math

import jax
import jax.numpy as jnp
from jax import lax
from jax.experimental import pallas as pl
from jax.experimental.pallas import tpu as pltpu
from jax.sharding import PartitionSpec as P

HD = 128
TILE = 384
SPT = 4
KSLOT = 8
SCALE = 1.0 / math.sqrt(HD)
NT = (((1,), (1,)), ((), ()))
TN = (((0,), (0,)), ((), ()))


def with_halo(block, axis, dim):
    count = lax.axis_size(axis)
    forward = [(i, i + 1) for i in range(count - 1)]
    backward = [(target, source) for source, target in forward]
    low = lax.ppermute(block, axis, forward)
    high = lax.ppermute(block, axis, backward)
    return jnp.concatenate([low, block, high], axis=dim)


def from_behind(block, axis, distance):
    devices = range(lax.axis_size(axis))
    route = [(i - distance, i) for i in devices if i - distance in devices]
    return lax.ppermute(block, axis, route)


def lane_fold(x, op):
    parts = [x[:, j * HD : (j + 1) * HD] for j in range(x.shape[1] // HD)]
    return functools.reduce(op, parts)


def slot_rows(slots_ref, a, s):
    start = pl.multiple_of(slots_ref[a * KSLOT + s] * TILE, TILE)
    return pl.ds(start, TILE)


def forward_kernel(slots_ref, counts_ref, q_ref, k_ref, v_ref, o_ref, lse_ref, s_scr):
    a = pl.program_id(1)
    q = q_ref[...]
    count = counts_ref[a]
    rows = functools.partial(slot_rows, slots_ref, a)

    def score_pass(s, row_max):
        scores = lax.dot_general(
            q, k_ref[rows(s), :], NT, preferred_element_type=jnp.float32
        ) * SCALE
        s_scr[s] = scores
        return jnp.maximum(row_max, lane_fold(scores, jnp.maximum))

    row_max = lax.fori_loop(
        0, count, score_pass, jnp.full((TILE, HD), -jnp.inf, jnp.float32)
    )
    row_max = jnp.max(row_max, axis=1, keepdims=True)

    def exp_pass(s, carry):
        row_total, acc = carry
        e = jnp.exp(s_scr[s] - row_max)
        acc = acc + jnp.dot(
            e.astype(jnp.bfloat16), v_ref[rows(s), :], preferred_element_type=jnp.float32
        )
        return row_total + lane_fold(e, jnp.add), acc

    row_total, acc = lax.fori_loop(
        0, count, exp_pass,
        (jnp.zeros((TILE, HD), jnp.float32), jnp.zeros((TILE, HD), jnp.float32)),
    )
    row_total = jnp.sum(row_total, axis=1, keepdims=True)
    o_ref[...] = (acc * (1.0 / row_total)).astype(jnp.bfloat16)
    lse_ref[...] = jnp.broadcast_to(row_max + jnp.log(row_total), (TILE, HD))


def backward_kernel(
    slots_ref, counts_ref, q_ref, do_ref, o_ref, lse_ref, k_ref, v_ref,
    dq_ref, dk_ref, dv_ref,
):
    a = pl.program_id(1)

    @pl.when(a == 0)
    def _():
        dk_ref[...] = jnp.zeros_like(dk_ref)
        dv_ref[...] = jnp.zeros_like(dv_ref)

    q = q_ref[...]
    do = do_ref[...]
    lse = lse_ref[:, :1]
    delta = jnp.sum(
        do.astype(jnp.float32) * o_ref[...].astype(jnp.float32), axis=1, keepdims=True
    )
    count = counts_ref[a]
    rows = functools.partial(slot_rows, slots_ref, a)

    def grad_pass(s, dq_acc):
        r = rows(s)
        k = k_ref[r, :]
        scores = lax.dot_general(q, k, NT, preferred_element_type=jnp.float32) * SCALE
        w = jnp.exp(scores - lse)
        g = lax.dot_general(do, v_ref[r, :], NT, preferred_element_type=jnp.float32)
        ds = (w * (g - delta)).astype(jnp.bfloat16)
        dk_ref[r, :] += lax.dot_general(ds, q, TN, preferred_element_type=jnp.float32)
        dv_ref[r, :] += lax.dot_general(
            w.astype(jnp.bfloat16), do, TN, preferred_element_type=jnp.float32
        )
        return dq_acc + jnp.dot(ds, k, preferred_element_type=jnp.float32)

    dq = lax.fori_loop(0, count, grad_pass, jnp.zeros((TILE, HD), jnp.float32))
    dq_ref[...] = (dq * SCALE).astype(jnp.bfloat16)


def specs(row_count, ext_rows):
    tile_spec = pl.BlockSpec((TILE, HD), lambda h, a, sl, ct: (a, h))
    ext_spec = pl.BlockSpec((ext_rows, HD), lambda h, a, sl, ct: (0, h))
    return tile_spec, ext_spec


def attention_forward(slots, counts, queries, keys, values):
    row_count, col_count = queries.shape
    tile_spec, ext_spec = specs(row_count, keys.shape[0])
    return pl.pallas_call(
        forward_kernel,
        grid_spec=pltpu.PrefetchScalarGridSpec(
            num_scalar_prefetch=2,
            grid=(col_count // HD, row_count // TILE),
            in_specs=[tile_spec, ext_spec, ext_spec],
            out_specs=[tile_spec, tile_spec],
            scratch_shapes=[pltpu.VMEM((KSLOT, TILE, TILE), jnp.float32)],
        ),
        out_shape=[
            jax.ShapeDtypeStruct((row_count, col_count), jnp.bfloat16),
            jax.ShapeDtypeStruct((row_count, col_count), jnp.float32),
        ],
        compiler_params=pltpu.CompilerParams(
            dimension_semantics=("arbitrary", "arbitrary"),
            vmem_limit_bytes=48 * 1024 * 1024,
        ),
    )(slots, counts, queries, keys, values)


def attention_backward(slots, counts, queries, grads, out, lse, keys, values):
    row_count, col_count = queries.shape
    ext_rows = keys.shape[0]
    tile_spec, ext_spec = specs(row_count, ext_rows)
    return pl.pallas_call(
        backward_kernel,
        grid_spec=pltpu.PrefetchScalarGridSpec(
            num_scalar_prefetch=2,
            grid=(col_count // HD, row_count // TILE),
            in_specs=[tile_spec, tile_spec, tile_spec, tile_spec, ext_spec, ext_spec],
            out_specs=[tile_spec, ext_spec, ext_spec],
        ),
        out_shape=[
            jax.ShapeDtypeStruct((row_count, col_count), jnp.bfloat16),
            jax.ShapeDtypeStruct((ext_rows, col_count), jnp.float32),
            jax.ShapeDtypeStruct((ext_rows, col_count), jnp.float32),
        ],
        compiler_params=pltpu.CompilerParams(
            dimension_semantics=("arbitrary", "arbitrary"),
            vmem_limit_bytes=48 * 1024 * 1024,
        ),
    )(slots, counts, queries, grads, out, lse, keys, values)


def shards(queries, key_states, value_states, out_grads, pattern):
    row_count, col_count = queries.shape
    own_tiles = row_count // TILE
    first_tile = lax.axis_index("ctx") * own_tiles
    base_tile = first_tile - SPT
    rims = with_halo(jnp.stack((key_states, value_states)), "ctx", 1)
    grads_heads = lax.all_to_all(out_grads, "head", split_axis=1, concat_axis=0, tiled=True)
    listed = lax.dynamic_slice_in_dim(pattern, first_tile, own_tiles, 0)
    allowed = listed >= 0
    slots = jnp.where(allowed, listed - base_tile, 0).reshape(-1).astype(jnp.int32)
    counts = jnp.sum(allowed.astype(jnp.int32), axis=1)
    out, lse = attention_forward(slots, counts, queries, rims[0], rims[1])
    attended = lax.all_to_all(out, "head", split_axis=0, concat_axis=1, tiled=True)
    attended, queries = lax.optimization_barrier((attended, queries))
    dq, dk, dv = attention_backward(
        slots, counts, queries, grads_heads, out, lse, rims[0], rims[1]
    )
    parts = jnp.stack((dk, dv))
    own_part = parts[:, row_count : 2 * row_count]
    lower_part = parts[:, :row_count].astype(jnp.bfloat16)
    upper_part = parts[:, 2 * row_count :].astype(jnp.bfloat16)
    from_above = from_behind(lower_part, "ctx", -1).astype(jnp.float32)
    from_below = from_behind(upper_part, "ctx", 1).astype(jnp.float32)
    total = own_part + from_above + from_below
    key_grads = (total[0] * SCALE).astype(jnp.bfloat16)
    value_grads = total[1].astype(jnp.bfloat16)
    return (attended, dq, key_grads, value_grads)


def solution(mesh):
    return jax.shard_map(
        shards,
        mesh=mesh,
        in_specs=(
            P("ctx", "head"),
            P("ctx", "head"),
            P("ctx", "head"),
            P(("ctx", "head"), None),
            P(),
        ),
        out_specs=(P(("ctx", "head"), None), P("ctx", "head"), P("ctx", "head"), P("ctx", "head")),
        check_vma=False,
    )
```

```python
import functools
import math

import jax
import jax.numpy as jnp
from jax import lax
from jax.experimental import pallas as pl
from jax.experimental.pallas import tpu as pltpu
from jax.sharding import PartitionSpec as P

HD = 128
TILE = 384
SPT = 4
KSLOT = 8
SCALE = 1.0 / math.sqrt(HD)
NT = (((1,), (1,)), ((), ()))
TN = (((0,), (0,)), ((), ()))


def with_halo(block, axis, dim):
    count = lax.axis_size(axis)
    forward = [(i, i + 1) for i in range(count - 1)]
    backward = [(target, source) for source, target in forward]
    low = lax.ppermute(block, axis, forward)
    high = lax.ppermute(block, axis, backward)
    return jnp.concatenate([low, block, high], axis=dim)


def from_behind(block, axis, distance):
    devices = range(lax.axis_size(axis))
    route = [(i - distance, i) for i in devices if i - distance in devices]
    return lax.ppermute(block, axis, route)


def lane_fold(x, op):
    parts = [x[:, j * HD : (j + 1) * HD] for j in range(x.shape[1] // HD)]
    return functools.reduce(op, parts)


def slot_rows(slots_ref, a, s):
    start = pl.multiple_of(slots_ref[a * KSLOT + s] * TILE, TILE)
    return pl.ds(start, TILE)


def forward_kernel(slots_ref, counts_ref, q_ref, k_ref, v_ref, o_ref, lse_ref, s_scr):
    a = pl.program_id(1)
    q = q_ref[...]
    count = counts_ref[a]
    rows = functools.partial(slot_rows, slots_ref, a)

    def score_pass(s, row_max):
        scores = lax.dot_general(
            q, k_ref[rows(s), :], NT, preferred_element_type=jnp.float32
        ) * SCALE
        s_scr[s] = scores
        return jnp.maximum(row_max, lane_fold(scores, jnp.maximum))

    row_max = lax.fori_loop(
        0, count, score_pass, jnp.full((TILE, HD), -jnp.inf, jnp.float32)
    )
    row_max = jnp.max(row_max, axis=1, keepdims=True)

    def exp_pass(s, carry):
        row_total, acc = carry
        e = jnp.exp(s_scr[s] - row_max)
        acc = acc + jnp.dot(
            e.astype(jnp.bfloat16), v_ref[rows(s), :], preferred_element_type=jnp.float32
        )
        return row_total + lane_fold(e, jnp.add), acc

    row_total, acc = lax.fori_loop(
        0, count, exp_pass,
        (jnp.zeros((TILE, HD), jnp.float32), jnp.zeros((TILE, HD), jnp.float32)),
    )
    row_total = jnp.sum(row_total, axis=1, keepdims=True)
    o_ref[...] = (acc * (1.0 / row_total)).astype(jnp.bfloat16)
    lse_ref[...] = jnp.broadcast_to(row_max + jnp.log(row_total), (TILE, HD))


def make_backward_kernel(own):
    def backward_kernel(
        slots_ref, counts_ref, q_ref, do_ref, o_ref, lse_ref, k_ref, v_ref, *rest
    ):
        if own:
            dq_in_ref, dq_ref, dk_ref, dv_ref = rest
        else:
            dq_ref, dk_ref, dv_ref = rest
        a = pl.program_id(1)

        @pl.when(a == 0)
        def _():
            dk_ref[...] = jnp.zeros_like(dk_ref)
            dv_ref[...] = jnp.zeros_like(dv_ref)

        q = q_ref[...]
        do = do_ref[...]
        lse = lse_ref[:, :1]
        delta = jnp.sum(
            do.astype(jnp.float32) * o_ref[...].astype(jnp.float32), axis=1, keepdims=True
        )
        count = counts_ref[a]
        rows = functools.partial(slot_rows, slots_ref, a)

        def acc_rows(s):
            slot = slots_ref[a * KSLOT + s]
            if own:
                slot = slot - SPT
            else:
                slot = jnp.where(slot < SPT, slot, slot - SPT)
            return pl.ds(pl.multiple_of(slot * TILE, TILE), TILE)

        def grad_pass(s, dq_acc):
            r = rows(s)
            ar = acc_rows(s)
            k = k_ref[r, :]
            scores = lax.dot_general(q, k, NT, preferred_element_type=jnp.float32) * SCALE
            w = jnp.exp(scores - lse)
            g = lax.dot_general(do, v_ref[r, :], NT, preferred_element_type=jnp.float32)
            ds = (w * (g - delta)).astype(jnp.bfloat16)
            dk_ref[ar, :] += lax.dot_general(ds, q, TN, preferred_element_type=jnp.float32)
            dv_ref[ar, :] += lax.dot_general(
                w.astype(jnp.bfloat16), do, TN, preferred_element_type=jnp.float32
            )
            return dq_acc + jnp.dot(ds, k, preferred_element_type=jnp.float32)

        init = dq_in_ref[...] if own else jnp.zeros((TILE, HD), jnp.float32)
        dq = lax.fori_loop(0, count, grad_pass, init)
        if own:
            dq_ref[...] = (dq * SCALE).astype(jnp.bfloat16)
        else:
            dq_ref[...] = dq

    return backward_kernel


def specs(row_count, ext_rows):
    tile_spec = pl.BlockSpec((TILE, HD), lambda h, a, sl, ct: (a, h))
    ext_spec = pl.BlockSpec((ext_rows, HD), lambda h, a, sl, ct: (0, h))
    return tile_spec, ext_spec


def attention_forward(slots, counts, queries, keys, values):
    row_count, col_count = queries.shape
    tile_spec, ext_spec = specs(row_count, keys.shape[0])
    return pl.pallas_call(
        forward_kernel,
        grid_spec=pltpu.PrefetchScalarGridSpec(
            num_scalar_prefetch=2,
            grid=(col_count // HD, row_count // TILE),
            in_specs=[tile_spec, ext_spec, ext_spec],
            out_specs=[tile_spec, tile_spec],
            scratch_shapes=[pltpu.VMEM((KSLOT, TILE, TILE), jnp.float32)],
        ),
        out_shape=[
            jax.ShapeDtypeStruct((row_count, col_count), jnp.bfloat16),
            jax.ShapeDtypeStruct((row_count, col_count), jnp.float32),
        ],
        compiler_params=pltpu.CompilerParams(
            dimension_semantics=("arbitrary", "arbitrary"),
            vmem_limit_bytes=48 * 1024 * 1024,
        ),
    )(slots, counts, queries, keys, values)


def attention_backward(slots, counts, queries, grads, out, lse, keys, values, dq_in=None):
    row_count, col_count = queries.shape
    ext_rows = keys.shape[0]
    own = dq_in is not None
    acc_rows = row_count if own else ext_rows - row_count
    tile_spec, ext_spec = specs(row_count, ext_rows)
    acc_spec = pl.BlockSpec((acc_rows, HD), lambda h, a, sl, ct: (0, h))
    operands = [slots, counts, queries, grads, out, lse, keys, values]
    in_specs = [tile_spec, tile_spec, tile_spec, tile_spec, ext_spec, ext_spec]
    if own:
        operands.append(dq_in)
        in_specs.append(tile_spec)
    dq_type = jnp.bfloat16 if own else jnp.float32
    return pl.pallas_call(
        make_backward_kernel(own),
        grid_spec=pltpu.PrefetchScalarGridSpec(
            num_scalar_prefetch=2,
            grid=(col_count // HD, row_count // TILE),
            in_specs=in_specs,
            out_specs=[tile_spec, acc_spec, acc_spec],
        ),
        out_shape=[
            jax.ShapeDtypeStruct((row_count, col_count), dq_type),
            jax.ShapeDtypeStruct((acc_rows, col_count), jnp.float32),
            jax.ShapeDtypeStruct((acc_rows, col_count), jnp.float32),
        ],
        compiler_params=pltpu.CompilerParams(
            dimension_semantics=("arbitrary", "arbitrary"),
            vmem_limit_bytes=48 * 1024 * 1024,
        ),
    )(*operands)


def split_slots(listed, base_tile, first_tile, own_tiles):
    allowed = listed >= 0
    mine = allowed & (listed >= first_tile) & (listed < first_tile + own_tiles)
    near = allowed & ~mine
    slots = jnp.where(allowed, listed - base_tile, 0)
    lists = []
    for keep in (mine, near):
        order = jnp.argsort(~keep, axis=1, stable=True)
        picked = jnp.take_along_axis(slots, order, axis=1)
        lists.append((picked.reshape(-1).astype(jnp.int32), jnp.sum(keep.astype(jnp.int32), axis=1)))
    return lists


def shards(queries, key_states, value_states, out_grads, pattern):
    row_count, col_count = queries.shape
    own_tiles = row_count // TILE
    first_tile = lax.axis_index("ctx") * own_tiles
    base_tile = first_tile - SPT
    rims = with_halo(jnp.stack((key_states, value_states)), "ctx", 1)
    grads_heads = lax.all_to_all(out_grads, "head", split_axis=1, concat_axis=0, tiled=True)
    listed = lax.dynamic_slice_in_dim(pattern, first_tile, own_tiles, 0)
    allowed = listed >= 0
    slots = jnp.where(allowed, listed - base_tile, 0).reshape(-1).astype(jnp.int32)
    counts = jnp.sum(allowed.astype(jnp.int32), axis=1)
    out, lse = attention_forward(slots, counts, queries, rims[0], rims[1])
    attended = lax.all_to_all(out, "head", split_axis=0, concat_axis=1, tiled=True)
    (own_slots, own_counts), (near_slots, near_counts) = split_slots(
        listed, base_tile, first_tile, own_tiles
    )
    dq_part, dk_near, dv_near = attention_backward(
        near_slots, near_counts, queries, grads_heads, out, lse, rims[0], rims[1]
    )
    near = jnp.stack((dk_near, dv_near)).astype(jnp.bfloat16)
    lower_part = near[:, :row_count]
    upper_part = near[:, row_count:]
    dq, dk_own, dv_own = attention_backward(
        own_slots, own_counts, queries, grads_heads, out, lse, rims[0], rims[1], dq_part
    )
    own_part = jnp.stack((dk_own, dv_own))
    from_above = from_behind(lower_part, "ctx", -1).astype(jnp.float32)
    from_below = from_behind(upper_part, "ctx", 1).astype(jnp.float32)
    total = own_part + from_above + from_below
    key_grads = (total[0] * SCALE).astype(jnp.bfloat16)
    value_grads = total[1].astype(jnp.bfloat16)
    return (attended, dq, key_grads, value_grads)


def solution(mesh):
    return jax.shard_map(
        shards,
        mesh=mesh,
        in_specs=(
            P("ctx", "head"),
            P("ctx", "head"),
            P("ctx", "head"),
            P(("ctx", "head"), None),
            P(),
        ),
        out_specs=(P(("ctx", "head"), None), P("ctx", "head"), P("ctx", "head"), P("ctx", "head")),
        check_vma=False,
    )
```

```python
import functools
import math

import jax
import jax.numpy as jnp
from jax import lax
from jax.experimental import pallas as pl
from jax.experimental.pallas import tpu as pltpu
from jax.sharding import PartitionSpec as P

HD = 128
TILE = 384
SPT = 4
KSLOT = 8
SCALE = 1.0 / math.sqrt(HD)
NT = (((1,), (1,)), ((), ()))
TN = (((0,), (0,)), ((), ()))


def with_halo(block, axis):
    count = lax.axis_size(axis)
    forward = [(i, i + 1) for i in range(count - 1)]
    backward = [(target, source) for source, target in forward]
    low = lax.ppermute(block, axis, forward)
    high = lax.ppermute(block, axis, backward)
    return (low, block, high)


def from_behind(block, axis, distance):
    devices = range(lax.axis_size(axis))
    route = [(i - distance, i) for i in devices if i - distance in devices]
    return lax.ppermute(block, axis, route)


def lane_fold(x, op):
    parts = [x[:, j * HD : (j + 1) * HD] for j in range(x.shape[1] // HD)]
    return functools.reduce(op, parts)


def pick(slots_ref, a, s, refs):
    slot = slots_ref[a * KSLOT + s]
    region = slot // SPT
    start = pl.multiple_of((slot - region * SPT) * TILE, TILE)
    low, mid, high = (ref[pl.ds(start, TILE), :] for ref in refs)
    return jnp.where(region == 0, low, jnp.where(region == 1, mid, high))


def forward_kernel(
    slots_ref, counts_ref, q_ref, kl_ref, km_ref, kh_ref, vl_ref, vm_ref, vh_ref,
    o_ref, lse_ref, s_scr,
):
    a = pl.program_id(1)
    q = q_ref[...]
    count = counts_ref[a]
    key_of = lambda s: pick(slots_ref, a, s, (kl_ref, km_ref, kh_ref))
    value_of = lambda s: pick(slots_ref, a, s, (vl_ref, vm_ref, vh_ref))

    def score_pass(s, row_max):
        scores = lax.dot_general(
            q, key_of(s), NT, preferred_element_type=jnp.float32
        ) * SCALE
        s_scr[s] = scores
        return jnp.maximum(row_max, lane_fold(scores, jnp.maximum))

    row_max = lax.fori_loop(
        0, count, score_pass, jnp.full((TILE, HD), -jnp.inf, jnp.float32)
    )
    row_max = jnp.max(row_max, axis=1, keepdims=True)

    def exp_pass(s, carry):
        row_total, acc = carry
        e = jnp.exp(s_scr[s] - row_max)
        acc = acc + jnp.dot(
            e.astype(jnp.bfloat16), value_of(s), preferred_element_type=jnp.float32
        )
        return row_total + lane_fold(e, jnp.add), acc

    row_total, acc = lax.fori_loop(
        0, count, exp_pass,
        (jnp.zeros((TILE, HD), jnp.float32), jnp.zeros((TILE, HD), jnp.float32)),
    )
    row_total = jnp.sum(row_total, axis=1, keepdims=True)
    o_ref[...] = (acc * (1.0 / row_total)).astype(jnp.bfloat16)
    lse_ref[...] = jnp.broadcast_to(row_max + jnp.log(row_total), (TILE, HD))


def make_backward_kernel(own):
    def backward_kernel(
        slots_ref, counts_ref, q_ref, do_ref, o_ref, lse_ref,
        kl_ref, km_ref, kh_ref, vl_ref, vm_ref, vh_ref, *rest
    ):
        if own:
            dq_in_ref, dq_ref, dk_ref, dv_ref = rest
        else:
            dq_ref, dk_ref, dv_ref = rest
        a = pl.program_id(1)

        @pl.when(a == 0)
        def _():
            dk_ref[...] = jnp.zeros_like(dk_ref)
            dv_ref[...] = jnp.zeros_like(dv_ref)

        q = q_ref[...]
        do = do_ref[...]
        lse = lse_ref[:, :1]
        delta = jnp.sum(
            do.astype(jnp.float32) * o_ref[...].astype(jnp.float32), axis=1, keepdims=True
        )
        count = counts_ref[a]
        key_of = lambda s: pick(slots_ref, a, s, (kl_ref, km_ref, kh_ref))
        value_of = lambda s: pick(slots_ref, a, s, (vl_ref, vm_ref, vh_ref))

        def acc_rows(s):
            slot = slots_ref[a * KSLOT + s]
            if own:
                slot = slot - SPT
            else:
                slot = jnp.where(slot < SPT, slot, slot - SPT)
            return pl.ds(pl.multiple_of(slot * TILE, TILE), TILE)

        def grad_pass(s, dq_acc):
            ar = acc_rows(s)
            k = key_of(s)
            scores = lax.dot_general(q, k, NT, preferred_element_type=jnp.float32) * SCALE
            w = jnp.exp(scores - lse)
            g = lax.dot_general(do, value_of(s), NT, preferred_element_type=jnp.float32)
            ds = (w * (g - delta)).astype(jnp.bfloat16)
            dk_ref[ar, :] += lax.dot_general(ds, q, TN, preferred_element_type=jnp.float32)
            dv_ref[ar, :] += lax.dot_general(
                w.astype(jnp.bfloat16), do, TN, preferred_element_type=jnp.float32
            )
            return dq_acc + jnp.dot(ds, k, preferred_element_type=jnp.float32)

        init = dq_in_ref[...] if own else jnp.zeros((TILE, HD), jnp.float32)
        dq = lax.fori_loop(0, count, grad_pass, init)
        if own:
            dq_ref[...] = (dq * SCALE).astype(jnp.bfloat16)
        else:
            dq_ref[...] = dq

    return backward_kernel


def specs(row_count, ext_rows):
    tile_spec = pl.BlockSpec((TILE, HD), lambda h, a, sl, ct: (a, h))
    ext_spec = pl.BlockSpec((row_count, HD), lambda h, a, sl, ct: (0, h))
    return tile_spec, ext_spec


def attention_forward(slots, counts, queries, keys, values):
    row_count, col_count = queries.shape
    tile_spec, ext_spec = specs(row_count, None)
    return pl.pallas_call(
        forward_kernel,
        grid_spec=pltpu.PrefetchScalarGridSpec(
            num_scalar_prefetch=2,
            grid=(col_count // HD, row_count // TILE),
            in_specs=[tile_spec] + [ext_spec] * 6,
            out_specs=[tile_spec, tile_spec],
            scratch_shapes=[pltpu.VMEM((KSLOT, TILE, TILE), jnp.float32)],
        ),
        out_shape=[
            jax.ShapeDtypeStruct((row_count, col_count), jnp.bfloat16),
            jax.ShapeDtypeStruct((row_count, col_count), jnp.float32),
        ],
        compiler_params=pltpu.CompilerParams(
            dimension_semantics=("arbitrary", "arbitrary"),
            vmem_limit_bytes=48 * 1024 * 1024,
        ),
    )(slots, counts, queries, *keys, *values)


def attention_backward(slots, counts, queries, grads, out, lse, keys, values, dq_in=None):
    row_count, col_count = queries.shape
    ext_rows = 3 * row_count
    own = dq_in is not None
    acc_rows = row_count if own else ext_rows - row_count
    tile_spec, ext_spec = specs(row_count, ext_rows)
    acc_spec = pl.BlockSpec((acc_rows, HD), lambda h, a, sl, ct: (0, h))
    operands = [slots, counts, queries, grads, out, lse, *keys, *values]
    in_specs = [tile_spec] * 4 + [ext_spec] * 6
    if own:
        operands.append(dq_in)
        in_specs.append(tile_spec)
    dq_type = jnp.bfloat16 if own else jnp.float32
    return pl.pallas_call(
        make_backward_kernel(own),
        grid_spec=pltpu.PrefetchScalarGridSpec(
            num_scalar_prefetch=2,
            grid=(col_count // HD, row_count // TILE),
            in_specs=in_specs,
            out_specs=[tile_spec, acc_spec, acc_spec],
        ),
        out_shape=[
            jax.ShapeDtypeStruct((row_count, col_count), dq_type),
            jax.ShapeDtypeStruct((acc_rows, col_count), jnp.float32),
            jax.ShapeDtypeStruct((acc_rows, col_count), jnp.float32),
        ],
        compiler_params=pltpu.CompilerParams(
            dimension_semantics=("arbitrary", "arbitrary"),
            vmem_limit_bytes=48 * 1024 * 1024,
        ),
    )(*operands)


def split_slots(listed, base_tile, first_tile, own_tiles):
    allowed = listed >= 0
    mine = allowed & (listed >= first_tile) & (listed < first_tile + own_tiles)
    near = allowed & ~mine
    slots = jnp.where(allowed, listed - base_tile, 0)
    lists = []
    for keep in (mine, near):
        order = jnp.argsort(~keep, axis=1, stable=True)
        picked = jnp.take_along_axis(slots, order, axis=1)
        lists.append((picked.reshape(-1).astype(jnp.int32), jnp.sum(keep.astype(jnp.int32), axis=1)))
    return lists


def shards(queries, key_states, value_states, out_grads, pattern):
    row_count, col_count = queries.shape
    own_tiles = row_count // TILE
    first_tile = lax.axis_index("ctx") * own_tiles
    base_tile = first_tile - SPT
    keys = with_halo(key_states, "ctx")
    values = with_halo(value_states, "ctx")
    grads_heads = lax.all_to_all(out_grads, "head", split_axis=1, concat_axis=0, tiled=True)
    listed = lax.dynamic_slice_in_dim(pattern, first_tile, own_tiles, 0)
    allowed = listed >= 0
    slots = jnp.where(allowed, listed - base_tile, 0).reshape(-1).astype(jnp.int32)
    counts = jnp.sum(allowed.astype(jnp.int32), axis=1)
    out, lse = attention_forward(slots, counts, queries, keys, values)
    attended = lax.all_to_all(out, "head", split_axis=0, concat_axis=1, tiled=True)
    (own_slots, own_counts), (near_slots, near_counts) = split_slots(
        listed, base_tile, first_tile, own_tiles
    )
    dq_part, dk_near, dv_near = attention_backward(
        near_slots, near_counts, queries, grads_heads, out, lse, keys, values
    )
    near = jnp.stack((dk_near, dv_near)).astype(jnp.bfloat16)
    lower_part = near[:, :row_count]
    upper_part = near[:, row_count:]
    dq, dk_own, dv_own = attention_backward(
        own_slots, own_counts, queries, grads_heads, out, lse, keys, values, dq_part
    )
    own_part = jnp.stack((dk_own, dv_own))
    from_above = from_behind(lower_part, "ctx", -1).astype(jnp.float32)
    from_below = from_behind(upper_part, "ctx", 1).astype(jnp.float32)
    total = own_part + from_above + from_below
    key_grads = (total[0] * SCALE).astype(jnp.bfloat16)
    value_grads = total[1].astype(jnp.bfloat16)
    return (attended, dq, key_grads, value_grads)


def solution(mesh):
    return jax.shard_map(
        shards,
        mesh=mesh,
        in_specs=(
            P("ctx", "head"),
            P("ctx", "head"),
            P("ctx", "head"),
            P(("ctx", "head"), None),
            P(),
        ),
        out_specs=(P(("ctx", "head"), None), P("ctx", "head"), P("ctx", "head"), P("ctx", "head")),
        check_vma=False,
    )
```

```python
import functools
import math

import jax
import jax.numpy as jnp
from jax import lax
from jax.experimental import pallas as pl
from jax.experimental.pallas import tpu as pltpu
from jax.sharding import PartitionSpec as P

HD = 128
TILE = 384
SPT = 4
KSLOT = 8
SCALE = 1.0 / math.sqrt(HD)
NT = (((1,), (1,)), ((), ()))
TN = (((0,), (0,)), ((), ()))


def with_halo(block, axis):
    count = lax.axis_size(axis)
    forward = [(i, i + 1) for i in range(count - 1)]
    backward = [(target, source) for source, target in forward]
    low = lax.ppermute(block, axis, forward)
    high = lax.ppermute(block, axis, backward)
    return (low, block, high)


def from_behind(block, axis, distance):
    devices = range(lax.axis_size(axis))
    route = [(i - distance, i) for i in devices if i - distance in devices]
    return lax.ppermute(block, axis, route)


def lane_fold(x, op):
    parts = [x[:, j * HD : (j + 1) * HD] for j in range(x.shape[1] // HD)]
    return functools.reduce(op, parts)


def pick(slots_ref, a, s, refs):
    slot = slots_ref[a * KSLOT + s]
    region = slot // SPT
    start = pl.multiple_of((slot - region * SPT) * TILE, TILE)
    low, mid, high = (ref[pl.ds(start, TILE), :] for ref in refs)
    return jnp.where(region == 0, low, jnp.where(region == 1, mid, high))


def forward_kernel(
    slots_ref, counts_ref, q_ref, kl_ref, km_ref, kh_ref, vl_ref, vm_ref, vh_ref,
    o_ref, lse_ref, s_scr,
):
    a = pl.program_id(1)
    q = q_ref[...]
    count = counts_ref[a]
    key_of = lambda s: pick(slots_ref, a, s, (kl_ref, km_ref, kh_ref))
    value_of = lambda s: pick(slots_ref, a, s, (vl_ref, vm_ref, vh_ref))

    def score_pass(s, row_max):
        scores = lax.dot_general(
            q, key_of(s), NT, preferred_element_type=jnp.float32
        ) * SCALE
        s_scr[s] = scores
        return jnp.maximum(row_max, lane_fold(scores, jnp.maximum))

    row_max = lax.fori_loop(
        0, count, score_pass, jnp.full((TILE, HD), -jnp.inf, jnp.float32)
    )
    row_max = jnp.max(row_max, axis=1, keepdims=True)

    def exp_pass(s, carry):
        row_total, acc = carry
        e = jnp.exp(s_scr[s] - row_max)
        acc = acc + jnp.dot(
            e.astype(jnp.bfloat16), value_of(s), preferred_element_type=jnp.float32
        )
        return row_total + lane_fold(e, jnp.add), acc

    row_total, acc = lax.fori_loop(
        0, count, exp_pass,
        (jnp.zeros((TILE, HD), jnp.float32), jnp.zeros((TILE, HD), jnp.float32)),
    )
    row_total = jnp.sum(row_total, axis=1, keepdims=True)
    o_ref[...] = (acc * (1.0 / row_total)).astype(jnp.bfloat16)
    lse_ref[...] = jnp.broadcast_to(row_max + jnp.log(row_total), (TILE, HD))


def make_backward_kernel(own):
    def backward_kernel(
        slots_ref, counts_ref, q_ref, do_ref, o_ref, lse_ref,
        kl_ref, km_ref, kh_ref, vl_ref, vm_ref, vh_ref, *rest
    ):
        if own:
            dq_in_ref, dq_ref, dk_ref, dv_ref = rest
        else:
            dq_ref, low_ref, high_ref, dk_ref, dv_ref = rest
        a = pl.program_id(1)

        @pl.when(a == 0)
        def _():
            dk_ref[...] = jnp.zeros_like(dk_ref)
            dv_ref[...] = jnp.zeros_like(dv_ref)

        q = q_ref[...]
        do = do_ref[...]
        lse = lse_ref[:, :1]
        delta = jnp.sum(
            do.astype(jnp.float32) * o_ref[...].astype(jnp.float32), axis=1, keepdims=True
        )
        count = counts_ref[a]
        key_of = lambda s: pick(slots_ref, a, s, (kl_ref, km_ref, kh_ref))
        value_of = lambda s: pick(slots_ref, a, s, (vl_ref, vm_ref, vh_ref))

        def acc_rows(s):
            slot = slots_ref[a * KSLOT + s]
            if own:
                slot = slot - SPT
            else:
                slot = jnp.where(slot < SPT, slot, slot - SPT)
            return pl.ds(pl.multiple_of(slot * TILE, TILE), TILE)

        def grad_pass(s, dq_acc):
            ar = acc_rows(s)
            k = key_of(s)
            scores = lax.dot_general(q, k, NT, preferred_element_type=jnp.float32) * SCALE
            w = jnp.exp(scores - lse)
            g = lax.dot_general(do, value_of(s), NT, preferred_element_type=jnp.float32)
            ds = (w * (g - delta)).astype(jnp.bfloat16)
            dk_ref[ar, :] += lax.dot_general(ds, q, TN, preferred_element_type=jnp.float32)
            dv_ref[ar, :] += lax.dot_general(
                w.astype(jnp.bfloat16), do, TN, preferred_element_type=jnp.float32
            )
            return dq_acc + jnp.dot(ds, k, preferred_element_type=jnp.float32)

        init = dq_in_ref[...] if own else jnp.zeros((TILE, HD), jnp.float32)
        dq = lax.fori_loop(0, count, grad_pass, init)
        if own:
            dq_ref[...] = (dq * SCALE).astype(jnp.bfloat16)
        else:
            dq_ref[...] = dq
            half = dk_ref.shape[0] // 2

            @pl.when(a == pl.num_programs(1) - 1)
            def _():
                low_ref[0] = dk_ref[:half, :].astype(jnp.bfloat16)
                low_ref[1] = dv_ref[:half, :].astype(jnp.bfloat16)
                high_ref[0] = dk_ref[half:, :].astype(jnp.bfloat16)
                high_ref[1] = dv_ref[half:, :].astype(jnp.bfloat16)

    return backward_kernel


def specs(row_count, ext_rows):
    tile_spec = pl.BlockSpec((TILE, HD), lambda h, a, sl, ct: (a, h))
    ext_spec = pl.BlockSpec((row_count, HD), lambda h, a, sl, ct: (0, h))
    return tile_spec, ext_spec


def attention_forward(slots, counts, queries, keys, values):
    row_count, col_count = queries.shape
    tile_spec, ext_spec = specs(row_count, None)
    return pl.pallas_call(
        forward_kernel,
        grid_spec=pltpu.PrefetchScalarGridSpec(
            num_scalar_prefetch=2,
            grid=(col_count // HD, row_count // TILE),
            in_specs=[tile_spec] + [ext_spec] * 6,
            out_specs=[tile_spec, tile_spec],
            scratch_shapes=[pltpu.VMEM((KSLOT, TILE, TILE), jnp.float32)],
        ),
        out_shape=[
            jax.ShapeDtypeStruct((row_count, col_count), jnp.bfloat16),
            jax.ShapeDtypeStruct((row_count, col_count), jnp.float32),
        ],
        compiler_params=pltpu.CompilerParams(
            dimension_semantics=("arbitrary", "arbitrary"),
            vmem_limit_bytes=48 * 1024 * 1024,
        ),
    )(slots, counts, queries, *keys, *values)


def attention_backward(slots, counts, queries, grads, out, lse, keys, values, dq_in=None):
    row_count, col_count = queries.shape
    ext_rows = 3 * row_count
    own = dq_in is not None
    acc_rows = row_count if own else ext_rows - row_count
    tile_spec, ext_spec = specs(row_count, ext_rows)
    acc_spec = pl.BlockSpec((acc_rows, HD), lambda h, a, sl, ct: (0, h))
    operands = [slots, counts, queries, grads, out, lse, *keys, *values]
    in_specs = [tile_spec] * 4 + [ext_spec] * 6
    if own:
        operands.append(dq_in)
        in_specs.append(tile_spec)
    if own:
        out_specs = [tile_spec, acc_spec, acc_spec]
        out_shape = [
            jax.ShapeDtypeStruct((row_count, col_count), jnp.bfloat16),
            jax.ShapeDtypeStruct((acc_rows, col_count), jnp.float32),
            jax.ShapeDtypeStruct((acc_rows, col_count), jnp.float32),
        ]
        scratch = []
    else:
        rim_spec = pl.BlockSpec((2, row_count, HD), lambda h, a, sl, ct: (0, 0, h))
        out_specs = [tile_spec, rim_spec, rim_spec]
        out_shape = [
            jax.ShapeDtypeStruct((row_count, col_count), jnp.float32),
            jax.ShapeDtypeStruct((2, row_count, col_count), jnp.bfloat16),
            jax.ShapeDtypeStruct((2, row_count, col_count), jnp.bfloat16),
        ]
        scratch = [pltpu.VMEM((acc_rows, HD), jnp.float32)] * 2
    return pl.pallas_call(
        make_backward_kernel(own),
        grid_spec=pltpu.PrefetchScalarGridSpec(
            num_scalar_prefetch=2,
            grid=(col_count // HD, row_count // TILE),
            in_specs=in_specs,
            out_specs=out_specs,
            scratch_shapes=scratch,
        ),
        out_shape=out_shape,
        compiler_params=pltpu.CompilerParams(
            dimension_semantics=("arbitrary", "arbitrary"),
            vmem_limit_bytes=48 * 1024 * 1024,
        ),
    )(*operands)


def split_slots(listed, base_tile, first_tile, own_tiles):
    allowed = listed >= 0
    mine = allowed & (listed >= first_tile) & (listed < first_tile + own_tiles)
    near = allowed & ~mine
    slots = jnp.where(allowed, listed - base_tile, 0)
    lists = []
    for keep in (mine, near):
        order = jnp.argsort(~keep, axis=1, stable=True)
        picked = jnp.take_along_axis(slots, order, axis=1)
        lists.append((picked.reshape(-1).astype(jnp.int32), jnp.sum(keep.astype(jnp.int32), axis=1)))
    return lists


def shards(queries, key_states, value_states, out_grads, pattern):
    row_count, col_count = queries.shape
    own_tiles = row_count // TILE
    first_tile = lax.axis_index("ctx") * own_tiles
    base_tile = first_tile - SPT
    keys = with_halo(key_states, "ctx")
    values = with_halo(value_states, "ctx")
    grads_heads = lax.all_to_all(out_grads, "head", split_axis=1, concat_axis=0, tiled=True)
    listed = lax.dynamic_slice_in_dim(pattern, first_tile, own_tiles, 0)
    allowed = listed >= 0
    slots = jnp.where(allowed, listed - base_tile, 0).reshape(-1).astype(jnp.int32)
    counts = jnp.sum(allowed.astype(jnp.int32), axis=1)
    out, lse = attention_forward(slots, counts, queries, keys, values)
    attended = lax.all_to_all(out, "head", split_axis=0, concat_axis=1, tiled=True)
    (own_slots, own_counts), (near_slots, near_counts) = split_slots(
        listed, base_tile, first_tile, own_tiles
    )
    dq_part, lower_part, upper_part = attention_backward(
        near_slots, near_counts, queries, grads_heads, out, lse, keys, values
    )
    dq, dk_own, dv_own = attention_backward(
        own_slots, own_counts, queries, grads_heads, out, lse, keys, values, dq_part
    )
    own_part = jnp.stack((dk_own, dv_own))
    from_above = from_behind(lower_part, "ctx", -1).astype(jnp.float32)
    from_below = from_behind(upper_part, "ctx", 1).astype(jnp.float32)
    total = own_part + from_above + from_below
    key_grads = (total[0] * SCALE).astype(jnp.bfloat16)
    value_grads = total[1].astype(jnp.bfloat16)
    return (attended, dq, key_grads, value_grads)


def solution(mesh):
    return jax.shard_map(
        shards,
        mesh=mesh,
        in_specs=(
            P("ctx", "head"),
            P("ctx", "head"),
            P("ctx", "head"),
            P(("ctx", "head"), None),
            P(),
        ),
        out_specs=(P(("ctx", "head"), None), P("ctx", "head"), P("ctx", "head"), P("ctx", "head")),
        check_vma=False,
    )
```

```python
import functools
import math

import jax
import jax.numpy as jnp
from jax import lax
from jax.experimental import pallas as pl
from jax.experimental.pallas import tpu as pltpu
from jax.sharding import PartitionSpec as P

HD = 128
TILE = 384
SPT = 4
KSLOT = 8
SCALE = 1.0 / math.sqrt(HD)
NT = (((1,), (1,)), ((), ()))
TN = (((0,), (0,)), ((), ()))


def with_halo(block, axis):
    count = lax.axis_size(axis)
    forward = [(i, i + 1) for i in range(count - 1)]
    backward = [(target, source) for source, target in forward]
    low = lax.ppermute(block, axis, forward)
    high = lax.ppermute(block, axis, backward)
    return (low, block, high)


def from_behind(block, axis, distance):
    devices = range(lax.axis_size(axis))
    route = [(i - distance, i) for i in devices if i - distance in devices]
    return lax.ppermute(block, axis, route)


def lane_fold(x, op):
    parts = [x[:, j * HD : (j + 1) * HD] for j in range(x.shape[1] // HD)]
    return functools.reduce(op, parts)


def pick(slots_ref, a, s, refs):
    slot = slots_ref[a * KSLOT + s]
    region = slot // SPT
    start = pl.multiple_of((slot - region * SPT) * TILE, TILE)
    low, mid, high = (ref[pl.ds(start, TILE), :] for ref in refs)
    return jnp.where(region == 0, low, jnp.where(region == 1, mid, high))


def forward_kernel(
    slots_ref, counts_ref, q_ref, kl_ref, km_ref, kh_ref, vl_ref, vm_ref, vh_ref,
    o_ref, lse_ref, s_scr,
):
    a = pl.program_id(1)
    q = q_ref[...]
    count = counts_ref[a]
    key_of = lambda s: pick(slots_ref, a, s, (kl_ref, km_ref, kh_ref))
    value_of = lambda s: pick(slots_ref, a, s, (vl_ref, vm_ref, vh_ref))

    def score_pass(s, row_max):
        scores = lax.dot_general(
            q, key_of(s), NT, preferred_element_type=jnp.float32
        ) * SCALE
        s_scr[s] = scores
        return jnp.maximum(row_max, lane_fold(scores, jnp.maximum))

    row_max = lax.fori_loop(
        0, count, score_pass, jnp.full((TILE, HD), -jnp.inf, jnp.float32)
    )
    row_max = jnp.max(row_max, axis=1, keepdims=True)

    def exp_pass(s, carry):
        row_total, acc = carry
        e = jnp.exp(s_scr[s] - row_max)
        acc = acc + jnp.dot(
            e.astype(jnp.bfloat16), value_of(s), preferred_element_type=jnp.float32
        )
        return row_total + lane_fold(e, jnp.add), acc

    row_total, acc = lax.fori_loop(
        0, count, exp_pass,
        (jnp.zeros((TILE, HD), jnp.float32), jnp.zeros((TILE, HD), jnp.float32)),
    )
    row_total = jnp.sum(row_total, axis=1, keepdims=True)
    o_ref[...] = (acc * (1.0 / row_total)).astype(jnp.bfloat16)
    lse_ref[...] = jnp.broadcast_to(row_max + jnp.log(row_total), (TILE, HD))


def make_backward_kernel(own):
    def backward_kernel(
        slots_ref, counts_ref, q_ref, do_ref, o_ref, lse_ref,
        kl_ref, km_ref, kh_ref, vl_ref, vm_ref, vh_ref, *rest
    ):
        if own:
            dq_in_ref, dq_ref, dk_ref, dv_ref = rest
        else:
            dq_ref, low_ref, high_ref, dk_ref, dv_ref = rest
        a = pl.program_id(1)

        @pl.when(a == 0)
        def _():
            dk_ref[...] = jnp.zeros_like(dk_ref)
            dv_ref[...] = jnp.zeros_like(dv_ref)

        q = q_ref[...]
        do = do_ref[...]
        lse = lse_ref[:, :1]
        delta = jnp.sum(
            do.astype(jnp.float32) * o_ref[...].astype(jnp.float32), axis=1, keepdims=True
        )
        count = counts_ref[a]
        key_of = lambda s: pick(slots_ref, a, s, (kl_ref, km_ref, kh_ref))
        value_of = lambda s: pick(slots_ref, a, s, (vl_ref, vm_ref, vh_ref))

        def acc_rows(s):
            slot = slots_ref[a * KSLOT + s]
            if own:
                slot = slot - SPT
            else:
                slot = jnp.where(slot < SPT, slot, slot - SPT)
            return pl.ds(pl.multiple_of(slot * TILE, TILE), TILE)

        def grad_pass(s, dq_acc):
            ar = acc_rows(s)
            k = key_of(s)
            scores = lax.dot_general(q, k, NT, preferred_element_type=jnp.float32) * SCALE
            w = jnp.exp(scores - lse)
            g = lax.dot_general(do, value_of(s), NT, preferred_element_type=jnp.float32)
            ds = (w * (g - delta)).astype(jnp.bfloat16)
            dk_ref[ar, :] += lax.dot_general(ds, q, TN, preferred_element_type=jnp.float32)
            dv_ref[ar, :] += lax.dot_general(
                w.astype(jnp.bfloat16), do, TN, preferred_element_type=jnp.float32
            )
            return dq_acc + jnp.dot(ds, k, preferred_element_type=jnp.float32)

        init = dq_in_ref[...] if own else jnp.zeros((TILE, HD), jnp.float32)
        dq = lax.fori_loop(0, count, grad_pass, init)
        if own:
            dq_ref[...] = (dq * SCALE).astype(jnp.bfloat16)
        else:
            dq_ref[...] = dq
            half = dk_ref.shape[0] // 2

            @pl.when(a == pl.num_programs(1) - 1)
            def _():
                low_ref[0] = dk_ref[:half, :].astype(jnp.bfloat16)
                low_ref[1] = dv_ref[:half, :].astype(jnp.bfloat16)
                high_ref[0] = dk_ref[half:, :].astype(jnp.bfloat16)
                high_ref[1] = dv_ref[half:, :].astype(jnp.bfloat16)

    return backward_kernel


def specs(row_count, ext_rows):
    tile_spec = pl.BlockSpec((TILE, HD), lambda h, a, sl, ct: (a, h))
    ext_spec = pl.BlockSpec((row_count, HD), lambda h, a, sl, ct: (0, h))
    return tile_spec, ext_spec


def attention_forward(slots, counts, queries, keys, values):
    row_count, col_count = queries.shape
    tile_spec, ext_spec = specs(row_count, None)
    return pl.pallas_call(
        forward_kernel,
        grid_spec=pltpu.PrefetchScalarGridSpec(
            num_scalar_prefetch=2,
            grid=(col_count // HD, row_count // TILE),
            in_specs=[tile_spec] + [ext_spec] * 6,
            out_specs=[tile_spec, tile_spec],
            scratch_shapes=[pltpu.VMEM((KSLOT, TILE, TILE), jnp.float32)],
        ),
        out_shape=[
            jax.ShapeDtypeStruct((row_count, col_count), jnp.bfloat16),
            jax.ShapeDtypeStruct((row_count, col_count), jnp.float32),
        ],
        compiler_params=pltpu.CompilerParams(
            dimension_semantics=("arbitrary", "arbitrary"),
            vmem_limit_bytes=48 * 1024 * 1024,
        ),
    )(slots, counts, queries, *keys, *values)


def attention_backward(slots, counts, queries, grads, out, lse, keys, values, dq_in=None):
    row_count, col_count = queries.shape
    ext_rows = 3 * row_count
    own = dq_in is not None
    acc_rows = row_count if own else ext_rows - row_count
    tile_spec, ext_spec = specs(row_count, ext_rows)
    acc_spec = pl.BlockSpec((acc_rows, HD), lambda h, a, sl, ct: (0, h))
    operands = [slots, counts, queries, grads, out, lse, *keys, *values]
    in_specs = [tile_spec] * 4 + [ext_spec] * 6
    if own:
        operands.append(dq_in)
        in_specs.append(tile_spec)
    if own:
        out_specs = [tile_spec, acc_spec, acc_spec]
        out_shape = [
            jax.ShapeDtypeStruct((row_count, col_count), jnp.bfloat16),
            jax.ShapeDtypeStruct((acc_rows, col_count), jnp.float32),
            jax.ShapeDtypeStruct((acc_rows, col_count), jnp.float32),
        ]
        scratch = []
    else:
        rim_spec = pl.BlockSpec((2, row_count, HD), lambda h, a, sl, ct: (0, 0, h))
        out_specs = [tile_spec, rim_spec, rim_spec]
        out_shape = [
            jax.ShapeDtypeStruct((row_count, col_count), jnp.float32),
            jax.ShapeDtypeStruct((2, row_count, col_count), jnp.bfloat16),
            jax.ShapeDtypeStruct((2, row_count, col_count), jnp.bfloat16),
        ]
        scratch = [pltpu.VMEM((acc_rows, HD), jnp.float32)] * 2
    return pl.pallas_call(
        make_backward_kernel(own),
        grid_spec=pltpu.PrefetchScalarGridSpec(
            num_scalar_prefetch=2,
            grid=(col_count // HD, row_count // TILE),
            in_specs=in_specs,
            out_specs=out_specs,
            scratch_shapes=scratch,
        ),
        out_shape=out_shape,
        compiler_params=pltpu.CompilerParams(
            dimension_semantics=("arbitrary", "arbitrary"),
            vmem_limit_bytes=48 * 1024 * 1024,
        ),
    )(*operands)


def split_slots(listed, base_tile, first_tile, own_tiles):
    allowed = listed >= 0
    mine = allowed & (listed >= first_tile) & (listed < first_tile + own_tiles)
    near = allowed & ~mine
    slots = jnp.where(allowed, listed - base_tile, 0)
    lists = []
    for keep in (mine, near):
        order = jnp.argsort(~keep, axis=1, stable=True)
        picked = jnp.take_along_axis(slots, order, axis=1)
        lists.append((picked.reshape(-1).astype(jnp.int32), jnp.sum(keep.astype(jnp.int32), axis=1)))
    return lists


def shards(queries, key_states, value_states, out_grads, pattern):
    row_count, col_count = queries.shape
    own_tiles = row_count // TILE
    first_tile = lax.axis_index("ctx") * own_tiles
    base_tile = first_tile - SPT
    keys = with_halo(key_states, "ctx")
    values = with_halo(value_states, "ctx")
    out_grads, keys, values = lax.optimization_barrier((out_grads, keys, values))
    grads_heads = lax.all_to_all(out_grads, "head", split_axis=1, concat_axis=0, tiled=True)
    listed = lax.dynamic_slice_in_dim(pattern, first_tile, own_tiles, 0)
    allowed = listed >= 0
    slots = jnp.where(allowed, listed - base_tile, 0).reshape(-1).astype(jnp.int32)
    counts = jnp.sum(allowed.astype(jnp.int32), axis=1)
    out, lse = attention_forward(slots, counts, queries, keys, values)
    attended = lax.all_to_all(out, "head", split_axis=0, concat_axis=1, tiled=True)
    (own_slots, own_counts), (near_slots, near_counts) = split_slots(
        listed, base_tile, first_tile, own_tiles
    )
    dq_part, lower_part, upper_part = attention_backward(
        near_slots, near_counts, queries, grads_heads, out, lse, keys, values
    )
    dq, dk_own, dv_own = attention_backward(
        own_slots, own_counts, queries, grads_heads, out, lse, keys, values, dq_part
    )
    own_part = jnp.stack((dk_own, dv_own))
    from_above = from_behind(lower_part, "ctx", -1).astype(jnp.float32)
    from_below = from_behind(upper_part, "ctx", 1).astype(jnp.float32)
    total = own_part + from_above + from_below
    key_grads = (total[0] * SCALE).astype(jnp.bfloat16)
    value_grads = total[1].astype(jnp.bfloat16)
    return (attended, dq, key_grads, value_grads)


def solution(mesh):
    return jax.shard_map(
        shards,
        mesh=mesh,
        in_specs=(
            P("ctx", "head"),
            P("ctx", "head"),
            P("ctx", "head"),
            P(("ctx", "head"), None),
            P(),
        ),
        out_specs=(P(("ctx", "head"), None), P("ctx", "head"), P("ctx", "head"), P("ctx", "head")),
        check_vma=False,
    )
```

```python
import functools
import math

import jax
import jax.numpy as jnp
from jax import lax
from jax.experimental import pallas as pl
from jax.experimental.pallas import tpu as pltpu
from jax.sharding import PartitionSpec as P

HD = 128
TILE = 384
SPT = 4
KSLOT = 8
SCALE = 1.0 / math.sqrt(HD)
NT = (((1,), (1,)), ((), ()))
TN = (((0,), (0,)), ((), ()))


def with_halo(block, axis):
    count = lax.axis_size(axis)
    forward = [(i, i + 1) for i in range(count - 1)]
    backward = [(target, source) for source, target in forward]
    low = lax.ppermute(block, axis, forward)
    high = lax.ppermute(block, axis, backward)
    return (low, block, high)


def from_behind(block, axis, distance):
    devices = range(lax.axis_size(axis))
    route = [(i - distance, i) for i in devices if i - distance in devices]
    return lax.ppermute(block, axis, route)


def lane_fold(x, op):
    parts = [x[:, j * HD : (j + 1) * HD] for j in range(x.shape[1] // HD)]
    return functools.reduce(op, parts)


def pick(slots_ref, a, s, refs):
    slot = slots_ref[a * KSLOT + s]
    region = slot // SPT
    start = pl.multiple_of((slot - region * SPT) * TILE, TILE)
    low, mid, high = (ref[pl.ds(start, TILE), :] for ref in refs)
    return jnp.where(region == 0, low, jnp.where(region == 1, mid, high))


def forward_kernel(
    slots_ref, counts_ref, q_ref, kl_ref, km_ref, kh_ref, vl_ref, vm_ref, vh_ref,
    o_ref, lse_ref, s_scr,
):
    a = pl.program_id(1)
    q = q_ref[...]
    count = counts_ref[a]
    key_of = lambda s: pick(slots_ref, a, s, (kl_ref, km_ref, kh_ref))
    value_of = lambda s: pick(slots_ref, a, s, (vl_ref, vm_ref, vh_ref))

    def score_pass(s, row_max):
        scores = lax.dot_general(
            q, key_of(s), NT, preferred_element_type=jnp.float32
        ) * SCALE
        s_scr[s] = scores
        return jnp.maximum(row_max, lane_fold(scores, jnp.maximum))

    row_max = lax.fori_loop(
        0, count, score_pass, jnp.full((TILE, HD), -jnp.inf, jnp.float32)
    )
    row_max = jnp.max(row_max, axis=1, keepdims=True)

    def exp_pass(s, carry):
        row_total, acc = carry
        e = jnp.exp(s_scr[s] - row_max)
        acc = acc + jnp.dot(
            e.astype(jnp.bfloat16), value_of(s), preferred_element_type=jnp.float32
        )
        return row_total + lane_fold(e, jnp.add), acc

    row_total, acc = lax.fori_loop(
        0, count, exp_pass,
        (jnp.zeros((TILE, HD), jnp.float32), jnp.zeros((TILE, HD), jnp.float32)),
    )
    row_total = jnp.sum(row_total, axis=1, keepdims=True)
    o_ref[...] = (acc * (1.0 / row_total)).astype(jnp.bfloat16)
    lse_ref[...] = jnp.broadcast_to(row_max + jnp.log(row_total), (TILE, HD))


def make_backward_kernel(own):
    def backward_kernel(
        slots_ref, counts_ref, q_ref, do_ref, o_ref, lse_ref,
        kl_ref, km_ref, kh_ref, vl_ref, vm_ref, vh_ref, *rest
    ):
        if own:
            dq_in_ref, dq_ref, dk_ref, dv_ref, dkt_scr, dvt_scr = rest
        else:
            dq_ref, low_ref, high_ref, dkt_scr, dvt_scr = rest
        a = pl.program_id(1)

        @pl.when(a == 0)
        def _():
            dkt_scr[...] = jnp.zeros_like(dkt_scr)
            dvt_scr[...] = jnp.zeros_like(dvt_scr)

        q = q_ref[...]
        do = do_ref[...]
        q_t = q.astype(jnp.float32).T.astype(jnp.bfloat16)
        do_t = do.astype(jnp.float32).T.astype(jnp.bfloat16)
        lse = lse_ref[:, :1]
        delta = jnp.sum(
            do.astype(jnp.float32) * o_ref[...].astype(jnp.float32), axis=1, keepdims=True
        )
        count = counts_ref[a]
        key_of = lambda s: pick(slots_ref, a, s, (kl_ref, km_ref, kh_ref))
        value_of = lambda s: pick(slots_ref, a, s, (vl_ref, vm_ref, vh_ref))

        def acc_tile(s):
            slot = slots_ref[a * KSLOT + s]
            if own:
                return slot - SPT
            return jnp.where(slot < SPT, slot, slot - SPT)

        def grad_pass(s, dq_acc):
            t = acc_tile(s)
            k = key_of(s)
            scores = lax.dot_general(q, k, NT, preferred_element_type=jnp.float32) * SCALE
            w = jnp.exp(scores - lse)
            g = lax.dot_general(do, value_of(s), NT, preferred_element_type=jnp.float32)
            ds = (w * (g - delta)).astype(jnp.bfloat16)
            dkt_scr[t] += jnp.dot(q_t, ds, preferred_element_type=jnp.float32)
            dvt_scr[t] += jnp.dot(
                do_t, w.astype(jnp.bfloat16), preferred_element_type=jnp.float32
            )
            return dq_acc + jnp.dot(ds, k, preferred_element_type=jnp.float32)

        init = dq_in_ref[...] if own else jnp.zeros((TILE, HD), jnp.float32)
        dq = lax.fori_loop(0, count, grad_pass, init)
        if own:
            dq_ref[...] = (dq * SCALE).astype(jnp.bfloat16)
        else:
            dq_ref[...] = dq

        @pl.when(a == pl.num_programs(1) - 1)
        def _():
            for t in range(dkt_scr.shape[0]):
                dk_t = dkt_scr[t].T
                dv_t = dvt_scr[t].T
                if own:
                    dk_ref[t * TILE : (t + 1) * TILE, :] = dk_t
                    dv_ref[t * TILE : (t + 1) * TILE, :] = dv_t
                else:
                    side, u = (low_ref, t) if t < SPT else (high_ref, t - SPT)
                    side[0, u * TILE : (u + 1) * TILE, :] = dk_t.astype(jnp.bfloat16)
                    side[1, u * TILE : (u + 1) * TILE, :] = dv_t.astype(jnp.bfloat16)

    return backward_kernel


def specs(row_count, ext_rows):
    tile_spec = pl.BlockSpec((TILE, HD), lambda h, a, sl, ct: (a, h))
    ext_spec = pl.BlockSpec((row_count, HD), lambda h, a, sl, ct: (0, h))
    return tile_spec, ext_spec


def attention_forward(slots, counts, queries, keys, values):
    row_count, col_count = queries.shape
    tile_spec, ext_spec = specs(row_count, None)
    return pl.pallas_call(
        forward_kernel,
        grid_spec=pltpu.PrefetchScalarGridSpec(
            num_scalar_prefetch=2,
            grid=(col_count // HD, row_count // TILE),
            in_specs=[tile_spec] + [ext_spec] * 6,
            out_specs=[tile_spec, tile_spec],
            scratch_shapes=[pltpu.VMEM((KSLOT, TILE, TILE), jnp.float32)],
        ),
        out_shape=[
            jax.ShapeDtypeStruct((row_count, col_count), jnp.bfloat16),
            jax.ShapeDtypeStruct((row_count, col_count), jnp.float32),
        ],
        compiler_params=pltpu.CompilerParams(
            dimension_semantics=("arbitrary", "arbitrary"),
            vmem_limit_bytes=48 * 1024 * 1024,
        ),
    )(slots, counts, queries, *keys, *values)


def attention_backward(slots, counts, queries, grads, out, lse, keys, values, dq_in=None):
    row_count, col_count = queries.shape
    ext_rows = 3 * row_count
    own = dq_in is not None
    acc_rows = row_count if own else ext_rows - row_count
    tile_spec, ext_spec = specs(row_count, ext_rows)
    acc_spec = pl.BlockSpec((acc_rows, HD), lambda h, a, sl, ct: (0, h))
    operands = [slots, counts, queries, grads, out, lse, *keys, *values]
    in_specs = [tile_spec] * 4 + [ext_spec] * 6
    if own:
        operands.append(dq_in)
        in_specs.append(tile_spec)
    if own:
        out_specs = [tile_spec, acc_spec, acc_spec]
        out_shape = [
            jax.ShapeDtypeStruct((row_count, col_count), jnp.bfloat16),
            jax.ShapeDtypeStruct((acc_rows, col_count), jnp.float32),
            jax.ShapeDtypeStruct((acc_rows, col_count), jnp.float32),
        ]
        scratch = [pltpu.VMEM((SPT, HD, TILE), jnp.float32)] * 2
    else:
        rim_spec = pl.BlockSpec((2, row_count, HD), lambda h, a, sl, ct: (0, 0, h))
        out_specs = [tile_spec, rim_spec, rim_spec]
        out_shape = [
            jax.ShapeDtypeStruct((row_count, col_count), jnp.float32),
            jax.ShapeDtypeStruct((2, row_count, col_count), jnp.bfloat16),
            jax.ShapeDtypeStruct((2, row_count, col_count), jnp.bfloat16),
        ]
        scratch = [pltpu.VMEM((2 * SPT, HD, TILE), jnp.float32)] * 2
    return pl.pallas_call(
        make_backward_kernel(own),
        grid_spec=pltpu.PrefetchScalarGridSpec(
            num_scalar_prefetch=2,
            grid=(col_count // HD, row_count // TILE),
            in_specs=in_specs,
            out_specs=out_specs,
            scratch_shapes=scratch,
        ),
        out_shape=out_shape,
        compiler_params=pltpu.CompilerParams(
            dimension_semantics=("arbitrary", "arbitrary"),
            vmem_limit_bytes=48 * 1024 * 1024,
        ),
    )(*operands)


def split_slots(listed, base_tile, first_tile, own_tiles):
    allowed = listed >= 0
    mine = allowed & (listed >= first_tile) & (listed < first_tile + own_tiles)
    near = allowed & ~mine
    slots = jnp.where(allowed, listed - base_tile, 0)
    lists = []
    for keep in (mine, near):
        order = jnp.argsort(~keep, axis=1, stable=True)
        picked = jnp.take_along_axis(slots, order, axis=1)
        lists.append((picked.reshape(-1).astype(jnp.int32), jnp.sum(keep.astype(jnp.int32), axis=1)))
    return lists


def shards(queries, key_states, value_states, out_grads, pattern):
    row_count, col_count = queries.shape
    own_tiles = row_count // TILE
    first_tile = lax.axis_index("ctx") * own_tiles
    base_tile = first_tile - SPT
    keys = with_halo(key_states, "ctx")
    values = with_halo(value_states, "ctx")
    grads_heads = lax.all_to_all(out_grads, "head", split_axis=1, concat_axis=0, tiled=True)
    listed = lax.dynamic_slice_in_dim(pattern, first_tile, own_tiles, 0)
    allowed = listed >= 0
    slots = jnp.where(allowed, listed - base_tile, 0).reshape(-1).astype(jnp.int32)
    counts = jnp.sum(allowed.astype(jnp.int32), axis=1)
    out, lse = attention_forward(slots, counts, queries, keys, values)
    attended = lax.all_to_all(out, "head", split_axis=0, concat_axis=1, tiled=True)
    (own_slots, own_counts), (near_slots, near_counts) = split_slots(
        listed, base_tile, first_tile, own_tiles
    )
    dq_part, lower_part, upper_part = attention_backward(
        near_slots, near_counts, queries, grads_heads, out, lse, keys, values
    )
    dq, dk_own, dv_own = attention_backward(
        own_slots, own_counts, queries, grads_heads, out, lse, keys, values, dq_part
    )
    own_part = jnp.stack((dk_own, dv_own))
    from_above = from_behind(lower_part, "ctx", -1).astype(jnp.float32)
    from_below = from_behind(upper_part, "ctx", 1).astype(jnp.float32)
    total = own_part + from_above + from_below
    key_grads = (total[0] * SCALE).astype(jnp.bfloat16)
    value_grads = total[1].astype(jnp.bfloat16)
    return (attended, dq, key_grads, value_grads)


def solution(mesh):
    return jax.shard_map(
        shards,
        mesh=mesh,
        in_specs=(
            P("ctx", "head"),
            P("ctx", "head"),
            P("ctx", "head"),
            P(("ctx", "head"), None),
            P(),
        ),
        out_specs=(P(("ctx", "head"), None), P("ctx", "head"), P("ctx", "head"), P("ctx", "head")),
        check_vma=False,
    )
```

```python
import functools
import math

import jax
import jax.numpy as jnp
from jax import lax
from jax.experimental import pallas as pl
from jax.experimental.pallas import tpu as pltpu
from jax.sharding import PartitionSpec as P

HD = 128
TILE = 384
SPT = 4
KSLOT = 8
SCALE = 1.0 / math.sqrt(HD)
NT = (((1,), (1,)), ((), ()))
TN = (((0,), (0,)), ((), ()))


def with_halo(block, axis):
    count = lax.axis_size(axis)
    forward = [(i, i + 1) for i in range(count - 1)]
    backward = [(target, source) for source, target in forward]
    low = lax.ppermute(block, axis, forward)
    high = lax.ppermute(block, axis, backward)
    return (low, block, high)


def from_behind(block, axis, distance):
    devices = range(lax.axis_size(axis))
    route = [(i - distance, i) for i in devices if i - distance in devices]
    return lax.ppermute(block, axis, route)


def lane_fold(x, op):
    parts = [x[:, j * HD : (j + 1) * HD] for j in range(x.shape[1] // HD)]
    return functools.reduce(op, parts)


def pick(slots_ref, a, s, refs):
    slot = slots_ref[a * KSLOT + s]
    region = slot // SPT
    start = pl.multiple_of((slot - region * SPT) * TILE, TILE)
    low, mid, high = (ref[pl.ds(start, TILE), :] for ref in refs)
    return jnp.where(region == 0, low, jnp.where(region == 1, mid, high))


def make_forward_kernel(first):
    def forward_kernel(slots_ref, counts_ref, q_ref, *rest):
        if first:
            k_ref, v_ref, m_ref, l_ref, acc_ref, s_scr = rest

            def key_of(s):
                local = slots_ref[a * KSLOT + s] - SPT
                return k_ref[pl.ds(pl.multiple_of(local * TILE, TILE), TILE), :]

            def value_of(s):
                local = slots_ref[a * KSLOT + s] - SPT
                return v_ref[pl.ds(pl.multiple_of(local * TILE, TILE), TILE), :]
        else:
            (kl_ref, km_ref, kh_ref, vl_ref, vm_ref, vh_ref,
             m_in_ref, l_in_ref, acc_in_ref, o_ref, lse_ref, s_scr) = rest
            key_of = lambda s: pick(slots_ref, a, s, (kl_ref, km_ref, kh_ref))
            value_of = lambda s: pick(slots_ref, a, s, (vl_ref, vm_ref, vh_ref))
        a = pl.program_id(1)
        q = q_ref[...]
        count = counts_ref[a]

        def score_pass(s, row_max):
            scores = lax.dot_general(
                q, key_of(s), NT, preferred_element_type=jnp.float32
            ) * SCALE
            s_scr[s] = scores
            return jnp.maximum(row_max, lane_fold(scores, jnp.maximum))

        init_max = (
            jnp.full((TILE, HD), -jnp.inf, jnp.float32) if first else m_in_ref[...]
        )
        row_max = lax.fori_loop(0, count, score_pass, init_max)
        row_max = jnp.max(row_max, axis=1, keepdims=True)

        def exp_pass(s, carry):
            row_total, acc = carry
            e = jnp.exp(s_scr[s] - row_max)
            acc = acc + jnp.dot(
                e.astype(jnp.bfloat16), value_of(s), preferred_element_type=jnp.float32
            )
            return row_total + lane_fold(e, jnp.add), acc

        if first:
            init = (jnp.zeros((TILE, HD), jnp.float32), jnp.zeros((TILE, HD), jnp.float32))
        else:
            keep = jnp.exp(m_in_ref[:, :1] - row_max)
            init = (l_in_ref[...] * keep, acc_in_ref[...] * keep)
        row_total, acc = lax.fori_loop(0, count, exp_pass, init)
        if first:
            m_ref[...] = jnp.broadcast_to(row_max, (TILE, HD))
            l_ref[...] = row_total
            acc_ref[...] = acc
        else:
            row_total = jnp.sum(row_total, axis=1, keepdims=True)
            o_ref[...] = (acc * (1.0 / row_total)).astype(jnp.bfloat16)
            lse_ref[...] = jnp.broadcast_to(row_max + jnp.log(row_total), (TILE, HD))

    return forward_kernel


def make_backward_kernel(own):
    def backward_kernel(
        slots_ref, counts_ref, q_ref, do_ref, o_ref, lse_ref,
        kl_ref, km_ref, kh_ref, vl_ref, vm_ref, vh_ref, *rest
    ):
        if own:
            dq_in_ref, dq_ref, dk_ref, dv_ref = rest
        else:
            dq_ref, low_ref, high_ref, dk_ref, dv_ref = rest
        a = pl.program_id(1)

        @pl.when(a == 0)
        def _():
            dk_ref[...] = jnp.zeros_like(dk_ref)
            dv_ref[...] = jnp.zeros_like(dv_ref)

        q = q_ref[...]
        do = do_ref[...]
        lse = lse_ref[:, :1]
        delta = jnp.sum(
            do.astype(jnp.float32) * o_ref[...].astype(jnp.float32), axis=1, keepdims=True
        )
        count = counts_ref[a]
        key_of = lambda s: pick(slots_ref, a, s, (kl_ref, km_ref, kh_ref))
        value_of = lambda s: pick(slots_ref, a, s, (vl_ref, vm_ref, vh_ref))

        def acc_rows(s):
            slot = slots_ref[a * KSLOT + s]
            if own:
                slot = slot - SPT
            else:
                slot = jnp.where(slot < SPT, slot, slot - SPT)
            return pl.ds(pl.multiple_of(slot * TILE, TILE), TILE)

        def grad_pass(s, dq_acc):
            ar = acc_rows(s)
            k = key_of(s)
            scores = lax.dot_general(q, k, NT, preferred_element_type=jnp.float32) * SCALE
            w = jnp.exp(scores - lse)
            g = lax.dot_general(do, value_of(s), NT, preferred_element_type=jnp.float32)
            ds = (w * (g - delta)).astype(jnp.bfloat16)
            dk_ref[ar, :] += lax.dot_general(ds, q, TN, preferred_element_type=jnp.float32)
            dv_ref[ar, :] += lax.dot_general(
                w.astype(jnp.bfloat16), do, TN, preferred_element_type=jnp.float32
            )
            return dq_acc + jnp.dot(ds, k, preferred_element_type=jnp.float32)

        init = dq_in_ref[...] if own else jnp.zeros((TILE, HD), jnp.float32)
        dq = lax.fori_loop(0, count, grad_pass, init)
        if own:
            dq_ref[...] = (dq * SCALE).astype(jnp.bfloat16)
        else:
            dq_ref[...] = dq
            half = dk_ref.shape[0] // 2

            @pl.when(a == pl.num_programs(1) - 1)
            def _():
                low_ref[0] = dk_ref[:half, :].astype(jnp.bfloat16)
                low_ref[1] = dv_ref[:half, :].astype(jnp.bfloat16)
                high_ref[0] = dk_ref[half:, :].astype(jnp.bfloat16)
                high_ref[1] = dv_ref[half:, :].astype(jnp.bfloat16)

    return backward_kernel


def specs(row_count, ext_rows):
    tile_spec = pl.BlockSpec((TILE, HD), lambda h, a, sl, ct: (a, h))
    ext_spec = pl.BlockSpec((row_count, HD), lambda h, a, sl, ct: (0, h))
    return tile_spec, ext_spec


def attention_forward(slots, counts, queries, keys, values, carry=None):
    row_count, col_count = queries.shape
    tile_spec, ext_spec = specs(row_count, None)
    first = carry is None
    if first:
        operands = [slots, counts, queries, keys, values]
        in_specs = [tile_spec, ext_spec, ext_spec]
        out_types = [jnp.float32] * 3
    else:
        operands = [slots, counts, queries, *keys, *values, *carry]
        in_specs = [tile_spec] + [ext_spec] * 6 + [tile_spec] * 3
        out_types = [jnp.bfloat16, jnp.float32]
    return pl.pallas_call(
        make_forward_kernel(first),
        grid_spec=pltpu.PrefetchScalarGridSpec(
            num_scalar_prefetch=2,
            grid=(col_count // HD, row_count // TILE),
            in_specs=in_specs,
            out_specs=[tile_spec] * len(out_types),
            scratch_shapes=[pltpu.VMEM((KSLOT, TILE, TILE), jnp.float32)],
        ),
        out_shape=[jax.ShapeDtypeStruct((row_count, col_count), t) for t in out_types],
        compiler_params=pltpu.CompilerParams(
            dimension_semantics=("arbitrary", "arbitrary"),
            vmem_limit_bytes=48 * 1024 * 1024,
        ),
    )(*operands)


def attention_backward(slots, counts, queries, grads, out, lse, keys, values, dq_in=None):
    row_count, col_count = queries.shape
    ext_rows = 3 * row_count
    own = dq_in is not None
    acc_rows = row_count if own else ext_rows - row_count
    tile_spec, ext_spec = specs(row_count, ext_rows)
    acc_spec = pl.BlockSpec((acc_rows, HD), lambda h, a, sl, ct: (0, h))
    operands = [slots, counts, queries, grads, out, lse, *keys, *values]
    in_specs = [tile_spec] * 4 + [ext_spec] * 6
    if own:
        operands.append(dq_in)
        in_specs.append(tile_spec)
    if own:
        out_specs = [tile_spec, acc_spec, acc_spec]
        out_shape = [
            jax.ShapeDtypeStruct((row_count, col_count), jnp.bfloat16),
            jax.ShapeDtypeStruct((acc_rows, col_count), jnp.float32),
            jax.ShapeDtypeStruct((acc_rows, col_count), jnp.float32),
        ]
        scratch = []
    else:
        rim_spec = pl.BlockSpec((2, row_count, HD), lambda h, a, sl, ct: (0, 0, h))
        out_specs = [tile_spec, rim_spec, rim_spec]
        out_shape = [
            jax.ShapeDtypeStruct((row_count, col_count), jnp.float32),
            jax.ShapeDtypeStruct((2, row_count, col_count), jnp.bfloat16),
            jax.ShapeDtypeStruct((2, row_count, col_count), jnp.bfloat16),
        ]
        scratch = [pltpu.VMEM((acc_rows, HD), jnp.float32)] * 2
    return pl.pallas_call(
        make_backward_kernel(own),
        grid_spec=pltpu.PrefetchScalarGridSpec(
            num_scalar_prefetch=2,
            grid=(col_count // HD, row_count // TILE),
            in_specs=in_specs,
            out_specs=out_specs,
            scratch_shapes=scratch,
        ),
        out_shape=out_shape,
        compiler_params=pltpu.CompilerParams(
            dimension_semantics=("arbitrary", "arbitrary"),
            vmem_limit_bytes=48 * 1024 * 1024,
        ),
    )(*operands)


def split_slots(listed, base_tile, first_tile, own_tiles):
    allowed = listed >= 0
    mine = allowed & (listed >= first_tile) & (listed < first_tile + own_tiles)
    near = allowed & ~mine
    slots = jnp.where(allowed, listed - base_tile, 0)
    lists = []
    for keep in (mine, near):
        order = jnp.argsort(~keep, axis=1, stable=True)
        picked = jnp.take_along_axis(slots, order, axis=1)
        lists.append((picked.reshape(-1).astype(jnp.int32), jnp.sum(keep.astype(jnp.int32), axis=1)))
    return lists


def shards(queries, key_states, value_states, out_grads, pattern):
    row_count, col_count = queries.shape
    own_tiles = row_count // TILE
    first_tile = lax.axis_index("ctx") * own_tiles
    base_tile = first_tile - SPT
    keys = with_halo(key_states, "ctx")
    values = with_halo(value_states, "ctx")
    grads_heads = lax.all_to_all(out_grads, "head", split_axis=1, concat_axis=0, tiled=True)
    listed = lax.dynamic_slice_in_dim(pattern, first_tile, own_tiles, 0)
    (own_slots, own_counts), (near_slots, near_counts) = split_slots(
        listed, base_tile, first_tile, own_tiles
    )
    carry = attention_forward(own_slots, own_counts, queries, key_states, value_states)
    out, lse = attention_forward(
        near_slots, near_counts, queries, keys, values, carry
    )
    attended = lax.all_to_all(out, "head", split_axis=0, concat_axis=1, tiled=True)
    dq_part, lower_part, upper_part = attention_backward(
        near_slots, near_counts, queries, grads_heads, out, lse, keys, values
    )
    dq, dk_own, dv_own = attention_backward(
        own_slots, own_counts, queries, grads_heads, out, lse, keys, values, dq_part
    )
    own_part = jnp.stack((dk_own, dv_own))
    from_above = from_behind(lower_part, "ctx", -1).astype(jnp.float32)
    from_below = from_behind(upper_part, "ctx", 1).astype(jnp.float32)
    total = own_part + from_above + from_below
    key_grads = (total[0] * SCALE).astype(jnp.bfloat16)
    value_grads = total[1].astype(jnp.bfloat16)
    return (attended, dq, key_grads, value_grads)


def solution(mesh):
    return jax.shard_map(
        shards,
        mesh=mesh,
        in_specs=(
            P("ctx", "head"),
            P("ctx", "head"),
            P("ctx", "head"),
            P(("ctx", "head"), None),
            P(),
        ),
        out_specs=(P(("ctx", "head"), None), P("ctx", "head"), P("ctx", "head"), P("ctx", "head")),
        check_vma=False,
    )
```

```python
import functools
import math

import jax
import jax.numpy as jnp
from jax import lax
from jax.experimental import pallas as pl
from jax.experimental.pallas import tpu as pltpu
from jax.sharding import PartitionSpec as P

HD = 128
TILE = 384
SPT = 4
KSLOT = 8
SCALE = 1.0 / math.sqrt(HD)
NT = (((1,), (1,)), ((), ()))
TN = (((0,), (0,)), ((), ()))


def with_halo(block, axis):
    count = lax.axis_size(axis)
    forward = [(i, i + 1) for i in range(count - 1)]
    backward = [(target, source) for source, target in forward]
    low = lax.ppermute(block, axis, forward)
    high = lax.ppermute(block, axis, backward)
    return (low, block, high)


def from_behind(block, axis, distance):
    devices = range(lax.axis_size(axis))
    route = [(i - distance, i) for i in devices if i - distance in devices]
    return lax.ppermute(block, axis, route)


def lane_fold(x, op):
    parts = [x[:, j * HD : (j + 1) * HD] for j in range(x.shape[1] // HD)]
    return functools.reduce(op, parts)


def pick(slots_ref, a, s, refs):
    slot = slots_ref[a * KSLOT + s]
    region = slot // SPT
    start = pl.multiple_of((slot - region * SPT) * TILE, TILE)
    low, mid, high = (ref[pl.ds(start, TILE), :] for ref in refs)
    return jnp.where(region == 0, low, jnp.where(region == 1, mid, high))


def make_forward_kernel(first):
    def forward_kernel(slots_ref, counts_ref, q_ref, *rest):
        if first:
            k_ref, v_ref, m_ref, l_ref, acc_ref, s_scr = rest

            def key_of(s):
                local = slots_ref[a * KSLOT + s] - SPT
                return k_ref[pl.ds(pl.multiple_of(local * TILE, TILE), TILE), :]

            def value_of(s):
                local = slots_ref[a * KSLOT + s] - SPT
                return v_ref[pl.ds(pl.multiple_of(local * TILE, TILE), TILE), :]
        else:
            (kl_ref, km_ref, kh_ref, vl_ref, vm_ref, vh_ref,
             m_in_ref, l_in_ref, acc_in_ref, o_ref, lse_ref, s_scr) = rest
            key_of = lambda s: pick(slots_ref, a, s, (kl_ref, km_ref, kh_ref))
            value_of = lambda s: pick(slots_ref, a, s, (vl_ref, vm_ref, vh_ref))
        a = pl.program_id(1)
        q = q_ref[...]
        count = counts_ref[a]

        def score_pass(s, row_max):
            scores = lax.dot_general(
                q, key_of(s), NT, preferred_element_type=jnp.float32
            ) * SCALE
            s_scr[s] = scores
            return jnp.maximum(row_max, lane_fold(scores, jnp.maximum))

        init_max = (
            jnp.full((TILE, HD), -jnp.inf, jnp.float32) if first else m_in_ref[...]
        )
        row_max = lax.fori_loop(0, count, score_pass, init_max)
        row_max = jnp.max(row_max, axis=1, keepdims=True)

        def exp_pass(s, carry):
            row_total, acc = carry
            e = jnp.exp(s_scr[s] - row_max)
            acc = acc + jnp.dot(
                e.astype(jnp.bfloat16), value_of(s), preferred_element_type=jnp.float32
            )
            return row_total + lane_fold(e, jnp.add), acc

        if first:
            init = (jnp.zeros((TILE, HD), jnp.float32), jnp.zeros((TILE, HD), jnp.float32))
        else:
            keep = jnp.exp(m_in_ref[:, :1] - row_max)
            init = (l_in_ref[...] * keep, acc_in_ref[...] * keep)
        row_total, acc = lax.fori_loop(0, count, exp_pass, init)
        if first:
            m_ref[...] = jnp.broadcast_to(row_max, (TILE, HD))
            l_ref[...] = row_total
            acc_ref[...] = acc
        else:
            row_total = jnp.sum(row_total, axis=1, keepdims=True)
            o_ref[...] = (acc * (1.0 / row_total)).astype(jnp.bfloat16)
            lse_ref[...] = jnp.broadcast_to(row_max + jnp.log(row_total), (TILE, HD))

    return forward_kernel


def make_backward_kernel(own):
    def backward_kernel(
        slots_ref, counts_ref, q_ref, do_ref, o_ref, lse_ref,
        kl_ref, km_ref, kh_ref, vl_ref, vm_ref, vh_ref, *rest
    ):
        if own:
            dq_in_ref, dq_ref, dk_ref, dv_ref = rest
        else:
            dq_ref, low_ref, high_ref, dk_ref, dv_ref = rest
        a = pl.program_id(1)

        @pl.when(a == 0)
        def _():
            dk_ref[...] = jnp.zeros_like(dk_ref)
            dv_ref[...] = jnp.zeros_like(dv_ref)

        q = q_ref[...]
        do = do_ref[...]
        lse = lse_ref[:, :1]
        delta = jnp.sum(
            do.astype(jnp.float32) * o_ref[...].astype(jnp.float32), axis=1, keepdims=True
        )
        count = counts_ref[a]
        key_of = lambda s: pick(slots_ref, a, s, (kl_ref, km_ref, kh_ref))
        value_of = lambda s: pick(slots_ref, a, s, (vl_ref, vm_ref, vh_ref))

        def acc_rows(s):
            slot = slots_ref[a * KSLOT + s]
            if own:
                slot = slot - SPT
            else:
                slot = jnp.where(slot < SPT, slot, slot - SPT)
            return pl.ds(pl.multiple_of(slot * TILE, TILE), TILE)

        def grad_pass(s, dq_acc):
            ar = acc_rows(s)
            k = key_of(s)
            scores = lax.dot_general(q, k, NT, preferred_element_type=jnp.float32) * SCALE
            w = jnp.exp(scores - lse)
            g = lax.dot_general(do, value_of(s), NT, preferred_element_type=jnp.float32)
            ds = (w * (g - delta)).astype(jnp.bfloat16)
            dk_ref[ar, :] += lax.dot_general(ds, q, TN, preferred_element_type=jnp.float32)
            dv_ref[ar, :] += lax.dot_general(
                w.astype(jnp.bfloat16), do, TN, preferred_element_type=jnp.float32
            )
            return dq_acc + jnp.dot(ds, k, preferred_element_type=jnp.float32)

        init = dq_in_ref[...] if own else jnp.zeros((TILE, HD), jnp.float32)
        dq = lax.fori_loop(0, count, grad_pass, init)
        if own:
            dq_ref[...] = (dq * SCALE).astype(jnp.bfloat16)
        else:
            dq_ref[...] = dq
            half = dk_ref.shape[0] // 2

            @pl.when(a == pl.num_programs(1) - 1)
            def _():
                low_ref[0] = dk_ref[:half, :].astype(jnp.bfloat16)
                low_ref[1] = dv_ref[:half, :].astype(jnp.bfloat16)
                high_ref[0] = dk_ref[half:, :].astype(jnp.bfloat16)
                high_ref[1] = dv_ref[half:, :].astype(jnp.bfloat16)

    return backward_kernel


def specs(row_count, ext_rows):
    tile_spec = pl.BlockSpec((TILE, HD), lambda h, a, sl, ct: (a, h))
    ext_spec = pl.BlockSpec((row_count, HD), lambda h, a, sl, ct: (0, h))
    return tile_spec, ext_spec


def attention_forward(slots, counts, queries, keys, values, carry=None):
    row_count, col_count = queries.shape
    tile_spec, ext_spec = specs(row_count, None)
    first = carry is None
    if first:
        operands = [slots, counts, queries, keys, values]
        in_specs = [tile_spec, ext_spec, ext_spec]
        out_types = [jnp.float32] * 3
    else:
        operands = [slots, counts, queries, *keys, *values, *carry]
        in_specs = [tile_spec] + [ext_spec] * 6 + [tile_spec] * 3
        out_types = [jnp.bfloat16, jnp.float32]
    return pl.pallas_call(
        make_forward_kernel(first),
        grid_spec=pltpu.PrefetchScalarGridSpec(
            num_scalar_prefetch=2,
            grid=(col_count // HD, row_count // TILE),
            in_specs=in_specs,
            out_specs=[tile_spec] * len(out_types),
            scratch_shapes=[pltpu.VMEM((KSLOT, TILE, TILE), jnp.float32)],
        ),
        out_shape=[jax.ShapeDtypeStruct((row_count, col_count), t) for t in out_types],
        compiler_params=pltpu.CompilerParams(
            dimension_semantics=("arbitrary", "arbitrary"),
            vmem_limit_bytes=48 * 1024 * 1024,
        ),
    )(*operands)


def attention_backward(slots, counts, queries, grads, out, lse, keys, values, dq_in=None):
    row_count, col_count = queries.shape
    ext_rows = 3 * row_count
    own = dq_in is not None
    acc_rows = row_count if own else ext_rows - row_count
    tile_spec, ext_spec = specs(row_count, ext_rows)
    acc_spec = pl.BlockSpec((acc_rows, HD), lambda h, a, sl, ct: (0, h))
    operands = [slots, counts, queries, grads, out, lse, *keys, *values]
    in_specs = [tile_spec] * 4 + [ext_spec] * 6
    if own:
        operands.append(dq_in)
        in_specs.append(tile_spec)
    if own:
        out_specs = [tile_spec, acc_spec, acc_spec]
        out_shape = [
            jax.ShapeDtypeStruct((row_count, col_count), jnp.bfloat16),
            jax.ShapeDtypeStruct((acc_rows, col_count), jnp.float32),
            jax.ShapeDtypeStruct((acc_rows, col_count), jnp.float32),
        ]
        scratch = []
    else:
        rim_spec = pl.BlockSpec((2, row_count, HD), lambda h, a, sl, ct: (0, 0, h))
        out_specs = [tile_spec, rim_spec, rim_spec]
        out_shape = [
            jax.ShapeDtypeStruct((row_count, col_count), jnp.float32),
            jax.ShapeDtypeStruct((2, row_count, col_count), jnp.bfloat16),
            jax.ShapeDtypeStruct((2, row_count, col_count), jnp.bfloat16),
        ]
        scratch = [pltpu.VMEM((acc_rows, HD), jnp.float32)] * 2
    return pl.pallas_call(
        make_backward_kernel(own),
        grid_spec=pltpu.PrefetchScalarGridSpec(
            num_scalar_prefetch=2,
            grid=(col_count // HD, row_count // TILE),
            in_specs=in_specs,
            out_specs=out_specs,
            scratch_shapes=scratch,
        ),
        out_shape=out_shape,
        compiler_params=pltpu.CompilerParams(
            dimension_semantics=("arbitrary", "arbitrary"),
            vmem_limit_bytes=48 * 1024 * 1024,
        ),
    )(*operands)


def split_slots(listed, base_tile, first_tile, own_tiles):
    allowed = listed >= 0
    mine = allowed & (listed >= first_tile) & (listed < first_tile + own_tiles)
    near = allowed & ~mine
    slots = jnp.where(allowed, listed - base_tile, 0)
    lists = []
    places = jnp.arange(listed.shape[1], dtype=jnp.int32)
    for keep in (mine, near):
        place = jnp.cumsum(keep.astype(jnp.int32), axis=1) - 1
        hit = keep[:, :, None] & (place[:, :, None] == places[None, None, :])
        picked = jnp.sum(jnp.where(hit, slots[:, :, None], 0), axis=1)
        lists.append((picked.reshape(-1).astype(jnp.int32), jnp.sum(keep.astype(jnp.int32), axis=1)))
    return lists


def shards(queries, key_states, value_states, out_grads, pattern):
    row_count, col_count = queries.shape
    own_tiles = row_count // TILE
    first_tile = lax.axis_index("ctx") * own_tiles
    base_tile = first_tile - SPT
    keys = with_halo(key_states, "ctx")
    values = with_halo(value_states, "ctx")
    grads_heads = lax.all_to_all(out_grads, "head", split_axis=1, concat_axis=0, tiled=True)
    listed = lax.dynamic_slice_in_dim(pattern, first_tile, own_tiles, 0)
    (own_slots, own_counts), (near_slots, near_counts) = split_slots(
        listed, base_tile, first_tile, own_tiles
    )
    carry = attention_forward(own_slots, own_counts, queries, key_states, value_states)
    out, lse = attention_forward(
        near_slots, near_counts, queries, keys, values, carry
    )
    attended = lax.all_to_all(out, "head", split_axis=0, concat_axis=1, tiled=True)
    dq_part, lower_part, upper_part = attention_backward(
        near_slots, near_counts, queries, grads_heads, out, lse, keys, values
    )
    dq, dk_own, dv_own = attention_backward(
        own_slots, own_counts, queries, grads_heads, out, lse, keys, values, dq_part
    )
    own_part = jnp.stack((dk_own, dv_own))
    from_above = from_behind(lower_part, "ctx", -1).astype(jnp.float32)
    from_below = from_behind(upper_part, "ctx", 1).astype(jnp.float32)
    total = own_part + from_above + from_below
    key_grads = (total[0] * SCALE).astype(jnp.bfloat16)
    value_grads = total[1].astype(jnp.bfloat16)
    return (attended, dq, key_grads, value_grads)


def solution(mesh):
    return jax.shard_map(
        shards,
        mesh=mesh,
        in_specs=(
            P("ctx", "head"),
            P("ctx", "head"),
            P("ctx", "head"),
            P(("ctx", "head"), None),
            P(),
        ),
        out_specs=(P(("ctx", "head"), None), P("ctx", "head"), P("ctx", "head"), P("ctx", "head")),
        check_vma=False,
    )
```

```python
import functools
import math

import jax
import jax.numpy as jnp
from jax import lax
from jax.experimental import pallas as pl
from jax.experimental.pallas import tpu as pltpu
from jax.sharding import PartitionSpec as P

HD = 128
TILE = 384
SPT = 4
KSLOT = 8
SCALE = 1.0 / math.sqrt(HD)
NT = (((1,), (1,)), ((), ()))
TN = (((0,), (0,)), ((), ()))


def with_halo(block, axis):
    count = lax.axis_size(axis)
    forward = [(i, i + 1) for i in range(count - 1)]
    backward = [(target, source) for source, target in forward]
    low = lax.ppermute(block, axis, forward)
    high = lax.ppermute(block, axis, backward)
    return (low, block, high)


def from_behind(block, axis, distance):
    devices = range(lax.axis_size(axis))
    route = [(i - distance, i) for i in devices if i - distance in devices]
    return lax.ppermute(block, axis, route)


def lane_fold(x, op):
    parts = [x[:, j * HD : (j + 1) * HD] for j in range(x.shape[1] // HD)]
    return functools.reduce(op, parts)


def pick(slots_ref, a, s, refs):
    slot = slots_ref[a * KSLOT + s]
    region = slot // SPT
    start = pl.multiple_of((slot - region * SPT) * TILE, TILE)
    low, mid, high = (ref[pl.ds(start, TILE), :] for ref in refs)
    return jnp.where(region == 0, low, jnp.where(region == 1, mid, high))


def make_forward_kernel(first):
    def forward_kernel(slots_ref, counts_ref, q_ref, *rest):
        if first:
            k_ref, v_ref, m_ref, l_ref, acc_ref, s_scr = rest

            def key_of(s):
                local = slots_ref[a * KSLOT + s] - SPT
                return k_ref[pl.ds(pl.multiple_of(local * TILE, TILE), TILE), :]

            def value_of(s):
                local = slots_ref[a * KSLOT + s] - SPT
                return v_ref[pl.ds(pl.multiple_of(local * TILE, TILE), TILE), :]
        else:
            (kl_ref, km_ref, kh_ref, vl_ref, vm_ref, vh_ref,
             m_in_ref, l_in_ref, acc_in_ref, o_ref, lse_ref, s_scr) = rest
            key_of = lambda s: pick(slots_ref, a, s, (kl_ref, km_ref, kh_ref))
            value_of = lambda s: pick(slots_ref, a, s, (vl_ref, vm_ref, vh_ref))
        a = pl.program_id(1)
        q = q_ref[...]
        count = counts_ref[a]

        def score_pass(s, row_max):
            scores = lax.dot_general(
                q, key_of(s), NT, preferred_element_type=jnp.float32
            ) * SCALE
            s_scr[s] = scores
            return jnp.maximum(row_max, lane_fold(scores, jnp.maximum))

        init_max = (
            jnp.full((TILE, HD), -jnp.inf, jnp.float32) if first else m_in_ref[...]
        )
        row_max = lax.fori_loop(0, count, score_pass, init_max)
        row_max = jnp.max(row_max, axis=1, keepdims=True)

        def exp_pass(s, carry):
            row_total, acc = carry
            e = jnp.exp(s_scr[s] - row_max)
            acc = acc + jnp.dot(
                e.astype(jnp.bfloat16), value_of(s), preferred_element_type=jnp.float32
            )
            return row_total + lane_fold(e, jnp.add), acc

        if first:
            init = (jnp.zeros((TILE, HD), jnp.float32), jnp.zeros((TILE, HD), jnp.float32))
        else:
            keep = jnp.exp(m_in_ref[:, :1] - row_max)
            init = (l_in_ref[...] * keep, acc_in_ref[...] * keep)
        row_total, acc = lax.fori_loop(0, count, exp_pass, init)
        if first:
            m_ref[...] = jnp.broadcast_to(row_max, (TILE, HD))
            l_ref[...] = row_total
            acc_ref[...] = acc
        else:
            row_total = jnp.sum(row_total, axis=1, keepdims=True)
            o_ref[...] = (acc * (1.0 / row_total)).astype(jnp.bfloat16)
            lse_ref[...] = jnp.broadcast_to(row_max + jnp.log(row_total), (TILE, HD))

    return forward_kernel


def make_backward_kernel(own):
    def backward_kernel(
        slots_ref, counts_ref, q_ref, do_ref, o_ref, lse_ref,
        kl_ref, km_ref, kh_ref, vl_ref, vm_ref, vh_ref, *rest
    ):
        if own:
            dq_in_ref, dq_ref, dk_ref, dv_ref, dkt_scr, dvt_scr = rest
        else:
            dq_ref, low_ref, high_ref, dkt_scr, dvt_scr = rest
        a = pl.program_id(1)

        @pl.when(a == 0)
        def _():
            dkt_scr[...] = jnp.zeros_like(dkt_scr)
            dvt_scr[...] = jnp.zeros_like(dvt_scr)

        q = q_ref[...]
        do = do_ref[...]
        q_t = q.astype(jnp.float32).T.astype(jnp.bfloat16)
        do_t = do.astype(jnp.float32).T.astype(jnp.bfloat16)
        lse = lse_ref[:, :1]
        delta = jnp.sum(
            do.astype(jnp.float32) * o_ref[...].astype(jnp.float32), axis=1, keepdims=True
        )
        count = counts_ref[a]
        key_of = lambda s: pick(slots_ref, a, s, (kl_ref, km_ref, kh_ref))
        value_of = lambda s: pick(slots_ref, a, s, (vl_ref, vm_ref, vh_ref))

        def acc_tile(s):
            slot = slots_ref[a * KSLOT + s]
            if own:
                return slot - SPT
            return jnp.where(slot < SPT, slot, slot - SPT)

        def grad_pass(s, dq_acc):
            t = acc_tile(s)
            k = key_of(s)
            scores = lax.dot_general(q, k, NT, preferred_element_type=jnp.float32) * SCALE
            w = jnp.exp(scores - lse)
            g = lax.dot_general(do, value_of(s), NT, preferred_element_type=jnp.float32)
            ds = (w * (g - delta)).astype(jnp.bfloat16)
            dkt_scr[t] += jnp.dot(q_t, ds, preferred_element_type=jnp.float32)
            dvt_scr[t] += jnp.dot(
                do_t, w.astype(jnp.bfloat16), preferred_element_type=jnp.float32
            )
            return dq_acc + jnp.dot(ds, k, preferred_element_type=jnp.float32)

        init = dq_in_ref[...] if own else jnp.zeros((TILE, HD), jnp.float32)
        dq = lax.fori_loop(0, count, grad_pass, init)
        if own:
            dq_ref[...] = (dq * SCALE).astype(jnp.bfloat16)
        else:
            dq_ref[...] = dq

        @pl.when(a == pl.num_programs(1) - 1)
        def _():
            for t in range(dkt_scr.shape[0]):
                dk_t = dkt_scr[t].T
                dv_t = dvt_scr[t].T
                if own:
                    dk_ref[t * TILE : (t + 1) * TILE, :] = dk_t
                    dv_ref[t * TILE : (t + 1) * TILE, :] = dv_t
                else:
                    side, u = (low_ref, t) if t < SPT else (high_ref, t - SPT)
                    side[0, u * TILE : (u + 1) * TILE, :] = dk_t.astype(jnp.bfloat16)
                    side[1, u * TILE : (u + 1) * TILE, :] = dv_t.astype(jnp.bfloat16)

    return backward_kernel


def specs(row_count, ext_rows):
    tile_spec = pl.BlockSpec((TILE, HD), lambda h, a, sl, ct: (a, h))
    ext_spec = pl.BlockSpec((row_count, HD), lambda h, a, sl, ct: (0, h))
    return tile_spec, ext_spec


def attention_forward(slots, counts, queries, keys, values, carry=None):
    row_count, col_count = queries.shape
    tile_spec, ext_spec = specs(row_count, None)
    first = carry is None
    if first:
        operands = [slots, counts, queries, keys, values]
        in_specs = [tile_spec, ext_spec, ext_spec]
        out_types = [jnp.float32] * 3
    else:
        operands = [slots, counts, queries, *keys, *values, *carry]
        in_specs = [tile_spec] + [ext_spec] * 6 + [tile_spec] * 3
        out_types = [jnp.bfloat16, jnp.float32]
    return pl.pallas_call(
        make_forward_kernel(first),
        grid_spec=pltpu.PrefetchScalarGridSpec(
            num_scalar_prefetch=2,
            grid=(col_count // HD, row_count // TILE),
            in_specs=in_specs,
            out_specs=[tile_spec] * len(out_types),
            scratch_shapes=[pltpu.VMEM((KSLOT, TILE, TILE), jnp.float32)],
        ),
        out_shape=[jax.ShapeDtypeStruct((row_count, col_count), t) for t in out_types],
        compiler_params=pltpu.CompilerParams(
            dimension_semantics=("arbitrary", "arbitrary"),
            vmem_limit_bytes=48 * 1024 * 1024,
        ),
    )(*operands)


def attention_backward(slots, counts, queries, grads, out, lse, keys, values, dq_in=None):
    row_count, col_count = queries.shape
    ext_rows = 3 * row_count
    own = dq_in is not None
    acc_rows = row_count if own else ext_rows - row_count
    tile_spec, ext_spec = specs(row_count, ext_rows)
    acc_spec = pl.BlockSpec((acc_rows, HD), lambda h, a, sl, ct: (0, h))
    operands = [slots, counts, queries, grads, out, lse, *keys, *values]
    in_specs = [tile_spec] * 4 + [ext_spec] * 6
    if own:
        operands.append(dq_in)
        in_specs.append(tile_spec)
    if own:
        out_specs = [tile_spec, acc_spec, acc_spec]
        out_shape = [
            jax.ShapeDtypeStruct((row_count, col_count), jnp.bfloat16),
            jax.ShapeDtypeStruct((acc_rows, col_count), jnp.float32),
            jax.ShapeDtypeStruct((acc_rows, col_count), jnp.float32),
        ]
        scratch = [pltpu.VMEM((SPT, HD, TILE), jnp.float32)] * 2
    else:
        rim_spec = pl.BlockSpec((2, row_count, HD), lambda h, a, sl, ct: (0, 0, h))
        out_specs = [tile_spec, rim_spec, rim_spec]
        out_shape = [
            jax.ShapeDtypeStruct((row_count, col_count), jnp.float32),
            jax.ShapeDtypeStruct((2, row_count, col_count), jnp.bfloat16),
            jax.ShapeDtypeStruct((2, row_count, col_count), jnp.bfloat16),
        ]
        scratch = [pltpu.VMEM((2 * SPT, HD, TILE), jnp.float32)] * 2
    return pl.pallas_call(
        make_backward_kernel(own),
        grid_spec=pltpu.PrefetchScalarGridSpec(
            num_scalar_prefetch=2,
            grid=(col_count // HD, row_count // TILE),
            in_specs=in_specs,
            out_specs=out_specs,
            scratch_shapes=scratch,
        ),
        out_shape=out_shape,
        compiler_params=pltpu.CompilerParams(
            dimension_semantics=("arbitrary", "arbitrary"),
            vmem_limit_bytes=48 * 1024 * 1024,
        ),
    )(*operands)


def split_slots(listed, base_tile, first_tile, own_tiles):
    allowed = listed >= 0
    mine = allowed & (listed >= first_tile) & (listed < first_tile + own_tiles)
    near = allowed & ~mine
    slots = jnp.where(allowed, listed - base_tile, 0)
    lists = []
    places = jnp.arange(listed.shape[1], dtype=jnp.int32)
    for keep in (mine, near):
        place = jnp.cumsum(keep.astype(jnp.int32), axis=1) - 1
        hit = keep[:, :, None] & (place[:, :, None] == places[None, None, :])
        picked = jnp.sum(jnp.where(hit, slots[:, :, None], 0), axis=1)
        lists.append((picked.reshape(-1).astype(jnp.int32), jnp.sum(keep.astype(jnp.int32), axis=1)))
    return lists


def shards(queries, key_states, value_states, out_grads, pattern):
    row_count, col_count = queries.shape
    own_tiles = row_count // TILE
    first_tile = lax.axis_index("ctx") * own_tiles
    base_tile = first_tile - SPT
    keys = with_halo(key_states, "ctx")
    values = with_halo(value_states, "ctx")
    grads_heads = lax.all_to_all(out_grads, "head", split_axis=1, concat_axis=0, tiled=True)
    listed = lax.dynamic_slice_in_dim(pattern, first_tile, own_tiles, 0)
    (own_slots, own_counts), (near_slots, near_counts) = split_slots(
        listed, base_tile, first_tile, own_tiles
    )
    carry = attention_forward(own_slots, own_counts, queries, key_states, value_states)
    out, lse = attention_forward(
        near_slots, near_counts, queries, keys, values, carry
    )
    attended = lax.all_to_all(out, "head", split_axis=0, concat_axis=1, tiled=True)
    dq_part, lower_part, upper_part = attention_backward(
        near_slots, near_counts, queries, grads_heads, out, lse, keys, values
    )
    dq, dk_own, dv_own = attention_backward(
        own_slots, own_counts, queries, grads_heads, out, lse, keys, values, dq_part
    )
    own_part = jnp.stack((dk_own, dv_own))
    from_above = from_behind(lower_part, "ctx", -1).astype(jnp.float32)
    from_below = from_behind(upper_part, "ctx", 1).astype(jnp.float32)
    total = own_part + from_above + from_below
    key_grads = (total[0] * SCALE).astype(jnp.bfloat16)
    value_grads = total[1].astype(jnp.bfloat16)
    return (attended, dq, key_grads, value_grads)


def solution(mesh):
    return jax.shard_map(
        shards,
        mesh=mesh,
        in_specs=(
            P("ctx", "head"),
            P("ctx", "head"),
            P("ctx", "head"),
            P(("ctx", "head"), None),
            P(),
        ),
        out_specs=(P(("ctx", "head"), None), P("ctx", "head"), P("ctx", "head"), P("ctx", "head")),
        check_vma=False,
    )
```

```python
import functools
import math

import jax
import jax.numpy as jnp
from jax import lax
from jax.experimental import pallas as pl
from jax.experimental.pallas import tpu as pltpu
from jax.sharding import PartitionSpec as P

HD = 128
TILE = 384
SPT = 4
KSLOT = 8
SCALE = 1.0 / math.sqrt(HD)
NT = (((1,), (1,)), ((), ()))
TN = (((0,), (0,)), ((), ()))


def with_halo(block, axis):
    count = lax.axis_size(axis)
    forward = [(i, i + 1) for i in range(count - 1)]
    backward = [(target, source) for source, target in forward]
    low = lax.ppermute(block, axis, forward)
    high = lax.ppermute(block, axis, backward)
    return (low, block, high)


def from_behind(block, axis, distance):
    devices = range(lax.axis_size(axis))
    route = [(i - distance, i) for i in devices if i - distance in devices]
    return lax.ppermute(block, axis, route)


def lane_fold(x, op):
    parts = [x[:, j * HD : (j + 1) * HD] for j in range(x.shape[1] // HD)]
    return functools.reduce(op, parts)


def pick(slots_ref, a, s, refs):
    slot = slots_ref[a * KSLOT + s]
    region = slot // SPT
    start = pl.multiple_of((slot - region * SPT) * TILE, TILE)
    low, mid, high = (ref[pl.ds(start, TILE), :] for ref in refs)
    return jnp.where(region == 0, low, jnp.where(region == 1, mid, high))


def make_forward_kernel(first):
    def forward_kernel(slots_ref, counts_ref, q_ref, *rest):
        if first:
            k_ref, v_ref, m_ref, l_ref, acc_ref, s_scr = rest

            def key_of(s):
                local = slots_ref[a * KSLOT + s] - SPT
                return k_ref[pl.ds(pl.multiple_of(local * TILE, TILE), TILE), :]

            def value_of(s):
                local = slots_ref[a * KSLOT + s] - SPT
                return v_ref[pl.ds(pl.multiple_of(local * TILE, TILE), TILE), :]
        else:
            (kl_ref, km_ref, kh_ref, vl_ref, vm_ref, vh_ref,
             m_in_ref, l_in_ref, acc_in_ref, o_ref, lse_ref, s_scr) = rest
            key_of = lambda s: pick(slots_ref, a, s, (kl_ref, km_ref, kh_ref))
            value_of = lambda s: pick(slots_ref, a, s, (vl_ref, vm_ref, vh_ref))
        a = pl.program_id(1)
        q = q_ref[...]
        count = counts_ref[a]

        def score_pass(s, row_max):
            scores = lax.dot_general(
                q, key_of(s), NT, preferred_element_type=jnp.float32
            ) * SCALE
            s_scr[s] = scores
            return jnp.maximum(row_max, lane_fold(scores, jnp.maximum))

        init_max = (
            jnp.full((TILE, HD), -jnp.inf, jnp.float32) if first else m_in_ref[...]
        )
        row_max = lax.fori_loop(0, count, score_pass, init_max)
        row_max = jnp.max(row_max, axis=1, keepdims=True)

        def exp_pass(s, carry):
            row_total, acc = carry
            e = jnp.exp(s_scr[s] - row_max)
            acc = acc + jnp.dot(
                e.astype(jnp.bfloat16), value_of(s), preferred_element_type=jnp.float32
            )
            return row_total + lane_fold(e, jnp.add), acc

        if first:
            init = (jnp.zeros((TILE, HD), jnp.float32), jnp.zeros((TILE, HD), jnp.float32))
        else:
            keep = jnp.exp(m_in_ref[:, :1] - row_max)
            init = (l_in_ref[...] * keep, acc_in_ref[...] * keep)
        row_total, acc = lax.fori_loop(0, count, exp_pass, init)
        if first:
            m_ref[...] = jnp.broadcast_to(row_max, (TILE, HD))
            l_ref[...] = row_total
            acc_ref[...] = acc
        else:
            row_total = jnp.sum(row_total, axis=1, keepdims=True)
            o_ref[...] = (acc * (1.0 / row_total)).astype(jnp.bfloat16)
            lse_ref[...] = jnp.broadcast_to(row_max + jnp.log(row_total), (TILE, HD))

    return forward_kernel


def make_backward_kernel(own):
    def backward_kernel(
        slots_ref, counts_ref, q_ref, do_ref, o_ref, lse_ref,
        kl_ref, km_ref, kh_ref, vl_ref, vm_ref, vh_ref, *rest
    ):
        if own:
            dq_in_ref, dq_ref, dk_ref, dv_ref = rest
        else:
            dq_ref, low_ref, high_ref, dk_ref, dv_ref = rest
        a = pl.program_id(1)

        @pl.when(a == 0)
        def _():
            dk_ref[...] = jnp.zeros_like(dk_ref)
            dv_ref[...] = jnp.zeros_like(dv_ref)

        q = q_ref[...]
        do = do_ref[...]
        lse = lse_ref[:, :1]
        delta = jnp.sum(
            do.astype(jnp.float32) * o_ref[...].astype(jnp.float32), axis=1, keepdims=True
        )
        count = counts_ref[a]
        key_of = lambda s: pick(slots_ref, a, s, (kl_ref, km_ref, kh_ref))
        value_of = lambda s: pick(slots_ref, a, s, (vl_ref, vm_ref, vh_ref))

        def acc_rows(s):
            slot = slots_ref[a * KSLOT + s]
            if own:
                slot = slot - SPT
            else:
                slot = jnp.where(slot < SPT, slot, slot - SPT)
            return pl.ds(pl.multiple_of(slot * TILE, TILE), TILE)

        def grad_pass(s, dq_acc):
            ar = acc_rows(s)
            k = key_of(s)
            scores = lax.dot_general(q, k, NT, preferred_element_type=jnp.float32) * SCALE
            w = jnp.exp(scores - lse)
            g = lax.dot_general(do, value_of(s), NT, preferred_element_type=jnp.float32)
            ds = (w * (g - delta)).astype(jnp.bfloat16)
            dk_ref[ar, :] += lax.dot_general(ds, q, TN, preferred_element_type=jnp.float32)
            dv_ref[ar, :] += lax.dot_general(
                w.astype(jnp.bfloat16), do, TN, preferred_element_type=jnp.float32
            )
            return dq_acc + jnp.dot(ds, k, preferred_element_type=jnp.float32)

        init = dq_in_ref[...] if own else jnp.zeros((TILE, HD), jnp.float32)
        dq = lax.fori_loop(0, count, grad_pass, init)
        if own:
            dq_ref[...] = (dq * SCALE).astype(jnp.bfloat16)
        else:
            dq_ref[...] = dq
            half = dk_ref.shape[0] // 2

            @pl.when(a == pl.num_programs(1) - 1)
            def _():
                low_ref[0] = dk_ref[:half, :].astype(jnp.bfloat16)
                low_ref[1] = dv_ref[:half, :].astype(jnp.bfloat16)
                high_ref[0] = dk_ref[half:, :].astype(jnp.bfloat16)
                high_ref[1] = dv_ref[half:, :].astype(jnp.bfloat16)

    return backward_kernel


def specs(row_count, ext_rows):
    tile_spec = pl.BlockSpec((TILE, HD), lambda h, a, sl, ct: (a, h))
    ext_spec = pl.BlockSpec((row_count, HD), lambda h, a, sl, ct: (0, h))
    return tile_spec, ext_spec


def attention_forward(slots, counts, queries, keys, values, carry=None):
    row_count, col_count = queries.shape
    tile_spec, ext_spec = specs(row_count, None)
    first = carry is None
    if first:
        operands = [slots, counts, queries, keys, values]
        in_specs = [tile_spec, ext_spec, ext_spec]
        out_types = [jnp.float32] * 3
    else:
        operands = [slots, counts, queries, *keys, *values, *carry]
        in_specs = [tile_spec] + [ext_spec] * 6 + [tile_spec] * 3
        out_types = [jnp.bfloat16, jnp.float32]
    return pl.pallas_call(
        make_forward_kernel(first),
        grid_spec=pltpu.PrefetchScalarGridSpec(
            num_scalar_prefetch=2,
            grid=(col_count // HD, row_count // TILE),
            in_specs=in_specs,
            out_specs=[tile_spec] * len(out_types),
            scratch_shapes=[pltpu.VMEM((KSLOT, TILE, TILE), jnp.float32)],
        ),
        out_shape=[jax.ShapeDtypeStruct((row_count, col_count), t) for t in out_types],
        compiler_params=pltpu.CompilerParams(
            dimension_semantics=("arbitrary", "arbitrary"),
            vmem_limit_bytes=48 * 1024 * 1024,
        ),
    )(*operands)


def attention_backward(slots, counts, queries, grads, out, lse, keys, values, dq_in=None):
    row_count, col_count = queries.shape
    ext_rows = 3 * row_count
    own = dq_in is not None
    acc_rows = row_count if own else ext_rows - row_count
    tile_spec, ext_spec = specs(row_count, ext_rows)
    acc_spec = pl.BlockSpec((acc_rows, HD), lambda h, a, sl, ct: (0, h))
    operands = [slots, counts, queries, grads, out, lse, *keys, *values]
    in_specs = [tile_spec] * 4 + [ext_spec] * 6
    if own:
        operands.append(dq_in)
        in_specs.append(tile_spec)
    if own:
        out_specs = [tile_spec, acc_spec, acc_spec]
        out_shape = [
            jax.ShapeDtypeStruct((row_count, col_count), jnp.bfloat16),
            jax.ShapeDtypeStruct((acc_rows, col_count), jnp.float32),
            jax.ShapeDtypeStruct((acc_rows, col_count), jnp.float32),
        ]
        scratch = []
    else:
        rim_spec = pl.BlockSpec((2, row_count, HD), lambda h, a, sl, ct: (0, 0, h))
        out_specs = [tile_spec, rim_spec, rim_spec]
        out_shape = [
            jax.ShapeDtypeStruct((row_count, col_count), jnp.float32),
            jax.ShapeDtypeStruct((2, row_count, col_count), jnp.bfloat16),
            jax.ShapeDtypeStruct((2, row_count, col_count), jnp.bfloat16),
        ]
        scratch = [pltpu.VMEM((acc_rows, HD), jnp.float32)] * 2
    return pl.pallas_call(
        make_backward_kernel(own),
        grid_spec=pltpu.PrefetchScalarGridSpec(
            num_scalar_prefetch=2,
            grid=(col_count // HD, row_count // TILE),
            in_specs=in_specs,
            out_specs=out_specs,
            scratch_shapes=scratch,
        ),
        out_shape=out_shape,
        compiler_params=pltpu.CompilerParams(
            dimension_semantics=("arbitrary", "arbitrary"),
            vmem_limit_bytes=48 * 1024 * 1024,
        ),
    )(*operands)


def split_slots(listed, base_tile, first_tile, own_tiles):
    allowed = listed >= 0
    mine = allowed & (listed >= first_tile) & (listed < first_tile + own_tiles)
    near = allowed & ~mine
    slots = jnp.where(allowed, listed - base_tile, 0)
    lists = []
    places = jnp.arange(listed.shape[1], dtype=jnp.int32)
    for keep in (mine, near):
        place = jnp.sum(
            keep[:, :, None] & (places[:, None] <= places[None, :])[None], axis=1
        ).astype(jnp.int32) - 1
        hit = keep[:, :, None] & (place[:, :, None] == places[None, None, :])
        picked = jnp.sum(jnp.where(hit, slots[:, :, None], 0), axis=1)
        lists.append((picked.reshape(-1).astype(jnp.int32), jnp.sum(keep.astype(jnp.int32), axis=1)))
    return lists


def shards(queries, key_states, value_states, out_grads, pattern):
    row_count, col_count = queries.shape
    own_tiles = row_count // TILE
    first_tile = lax.axis_index("ctx") * own_tiles
    base_tile = first_tile - SPT
    keys = with_halo(key_states, "ctx")
    values = with_halo(value_states, "ctx")
    grads_heads = lax.all_to_all(out_grads, "head", split_axis=1, concat_axis=0, tiled=True)
    listed = lax.dynamic_slice_in_dim(pattern, first_tile, own_tiles, 0)
    (own_slots, own_counts), (near_slots, near_counts) = split_slots(
        listed, base_tile, first_tile, own_tiles
    )
    carry = attention_forward(own_slots, own_counts, queries, key_states, value_states)
    out, lse = attention_forward(
        near_slots, near_counts, queries, keys, values, carry
    )
    attended = lax.all_to_all(out, "head", split_axis=0, concat_axis=1, tiled=True)
    dq_part, lower_part, upper_part = attention_backward(
        near_slots, near_counts, queries, grads_heads, out, lse, keys, values
    )
    dq, dk_own, dv_own = attention_backward(
        own_slots, own_counts, queries, grads_heads, out, lse, keys, values, dq_part
    )
    own_part = jnp.stack((dk_own, dv_own))
    from_above = from_behind(lower_part, "ctx", -1).astype(jnp.float32)
    from_below = from_behind(upper_part, "ctx", 1).astype(jnp.float32)
    total = own_part + from_above + from_below
    key_grads = (total[0] * SCALE).astype(jnp.bfloat16)
    value_grads = total[1].astype(jnp.bfloat16)
    return (attended, dq, key_grads, value_grads)


def solution(mesh):
    return jax.shard_map(
        shards,
        mesh=mesh,
        in_specs=(
            P("ctx", "head"),
            P("ctx", "head"),
            P("ctx", "head"),
            P(("ctx", "head"), None),
            P(),
        ),
        out_specs=(P(("ctx", "head"), None), P("ctx", "head"), P("ctx", "head"), P("ctx", "head")),
        check_vma=False,
    )
```

```python
import functools
import math

import jax
import jax.numpy as jnp
from jax import lax
from jax.experimental import pallas as pl
from jax.experimental.pallas import tpu as pltpu
from jax.sharding import PartitionSpec as P

HD = 128
TILE = 384
SPT = 4
KSLOT = 8
SCALE = 1.0 / math.sqrt(HD)
NT = (((1,), (1,)), ((), ()))
TN = (((0,), (0,)), ((), ()))


def with_halo(block, axis):
    count = lax.axis_size(axis)
    forward = [(i, i + 1) for i in range(count - 1)]
    backward = [(target, source) for source, target in forward]
    low = lax.ppermute(block, axis, forward)
    high = lax.ppermute(block, axis, backward)
    return (low, block, high)


def from_behind(block, axis, distance):
    devices = range(lax.axis_size(axis))
    route = [(i - distance, i) for i in devices if i - distance in devices]
    return lax.ppermute(block, axis, route)


def lane_fold(x, op):
    parts = [x[:, j * HD : (j + 1) * HD] for j in range(x.shape[1] // HD)]
    return functools.reduce(op, parts)


def pick(slots_ref, a, s, refs):
    slot = slots_ref[a * KSLOT + s]
    below = slot < SPT
    start = pl.multiple_of(jnp.where(below, slot, slot - 2 * SPT) * TILE, TILE)
    low, _, high = refs
    return jnp.where(below, low[pl.ds(start, TILE), :], high[pl.ds(start, TILE), :])


def pick_own(slots_ref, a, s, ref):
    start = pl.multiple_of((slots_ref[a * KSLOT + s] - SPT) * TILE, TILE)
    return ref[pl.ds(start, TILE), :]


def make_forward_kernel(first):
    def forward_kernel(slots_ref, counts_ref, q_ref, *rest):
        if first:
            k_ref, v_ref, m_ref, l_ref, acc_ref, s_scr = rest

            def key_of(s):
                local = slots_ref[a * KSLOT + s] - SPT
                return k_ref[pl.ds(pl.multiple_of(local * TILE, TILE), TILE), :]

            def value_of(s):
                local = slots_ref[a * KSLOT + s] - SPT
                return v_ref[pl.ds(pl.multiple_of(local * TILE, TILE), TILE), :]
        else:
            (kl_ref, km_ref, kh_ref, vl_ref, vm_ref, vh_ref,
             m_in_ref, l_in_ref, acc_in_ref, o_ref, lse_ref, s_scr) = rest
            key_of = lambda s: pick(slots_ref, a, s, (kl_ref, km_ref, kh_ref))
            value_of = lambda s: pick(slots_ref, a, s, (vl_ref, vm_ref, vh_ref))
        a = pl.program_id(1)
        q = q_ref[...]
        count = counts_ref[a]

        def score_pass(s, row_max):
            scores = lax.dot_general(
                q, key_of(s), NT, preferred_element_type=jnp.float32
            ) * SCALE
            s_scr[s] = scores
            return jnp.maximum(row_max, lane_fold(scores, jnp.maximum))

        init_max = (
            jnp.full((TILE, HD), -jnp.inf, jnp.float32) if first else m_in_ref[...]
        )
        row_max = lax.fori_loop(0, count, score_pass, init_max)
        row_max = jnp.max(row_max, axis=1, keepdims=True)

        def exp_pass(s, carry):
            row_total, acc = carry
            e = jnp.exp(s_scr[s] - row_max)
            acc = acc + jnp.dot(
                e.astype(jnp.bfloat16), value_of(s), preferred_element_type=jnp.float32
            )
            return row_total + lane_fold(e, jnp.add), acc

        if first:
            init = (jnp.zeros((TILE, HD), jnp.float32), jnp.zeros((TILE, HD), jnp.float32))
        else:
            keep = jnp.exp(m_in_ref[:, :1] - row_max)
            init = (l_in_ref[...] * keep, acc_in_ref[...] * keep)
        row_total, acc = lax.fori_loop(0, count, exp_pass, init)
        if first:
            m_ref[...] = jnp.broadcast_to(row_max, (TILE, HD))
            l_ref[...] = row_total
            acc_ref[...] = acc
        else:
            row_total = jnp.sum(row_total, axis=1, keepdims=True)
            o_ref[...] = (acc * (1.0 / row_total)).astype(jnp.bfloat16)
            lse_ref[...] = jnp.broadcast_to(row_max + jnp.log(row_total), (TILE, HD))

    return forward_kernel


def make_backward_kernel(own):
    def backward_kernel(
        slots_ref, counts_ref, q_ref, do_ref, o_ref, lse_ref,
        kl_ref, km_ref, kh_ref, vl_ref, vm_ref, vh_ref, *rest
    ):
        if own:
            dq_in_ref, dq_ref, dk_ref, dv_ref = rest
        else:
            dq_ref, low_ref, high_ref, dk_ref, dv_ref = rest
        a = pl.program_id(1)

        @pl.when(a == 0)
        def _():
            dk_ref[...] = jnp.zeros_like(dk_ref)
            dv_ref[...] = jnp.zeros_like(dv_ref)

        q = q_ref[...]
        do = do_ref[...]
        lse = lse_ref[:, :1]
        delta = jnp.sum(
            do.astype(jnp.float32) * o_ref[...].astype(jnp.float32), axis=1, keepdims=True
        )
        count = counts_ref[a]
        if own:
            key_of = lambda s: pick_own(slots_ref, a, s, km_ref)
            value_of = lambda s: pick_own(slots_ref, a, s, vm_ref)
        else:
            key_of = lambda s: pick(slots_ref, a, s, (kl_ref, km_ref, kh_ref))
            value_of = lambda s: pick(slots_ref, a, s, (vl_ref, vm_ref, vh_ref))

        def acc_rows(s):
            slot = slots_ref[a * KSLOT + s]
            if own:
                slot = slot - SPT
            else:
                slot = jnp.where(slot < SPT, slot, slot - SPT)
            return pl.ds(pl.multiple_of(slot * TILE, TILE), TILE)

        def grad_pass(s, dq_acc):
            ar = acc_rows(s)
            k = key_of(s)
            scores = lax.dot_general(q, k, NT, preferred_element_type=jnp.float32) * SCALE
            w = jnp.exp(scores - lse)
            g = lax.dot_general(do, value_of(s), NT, preferred_element_type=jnp.float32)
            ds = (w * (g - delta)).astype(jnp.bfloat16)
            dk_ref[ar, :] += lax.dot_general(ds, q, TN, preferred_element_type=jnp.float32)
            dv_ref[ar, :] += lax.dot_general(
                w.astype(jnp.bfloat16), do, TN, preferred_element_type=jnp.float32
            )
            return dq_acc + jnp.dot(ds, k, preferred_element_type=jnp.float32)

        init = dq_in_ref[...] if own else jnp.zeros((TILE, HD), jnp.float32)
        dq = lax.fori_loop(0, count, grad_pass, init)
        if own:
            dq_ref[...] = (dq * SCALE).astype(jnp.bfloat16)
        else:
            dq_ref[...] = dq
            half = dk_ref.shape[0] // 2

            @pl.when(a == pl.num_programs(1) - 1)
            def _():
                low_ref[0] = dk_ref[:half, :].astype(jnp.bfloat16)
                low_ref[1] = dv_ref[:half, :].astype(jnp.bfloat16)
                high_ref[0] = dk_ref[half:, :].astype(jnp.bfloat16)
                high_ref[1] = dv_ref[half:, :].astype(jnp.bfloat16)

    return backward_kernel


def specs(row_count, ext_rows):
    tile_spec = pl.BlockSpec((TILE, HD), lambda h, a, sl, ct: (a, h))
    ext_spec = pl.BlockSpec((row_count, HD), lambda h, a, sl, ct: (0, h))
    return tile_spec, ext_spec


def attention_forward(slots, counts, queries, keys, values, carry=None):
    row_count, col_count = queries.shape
    tile_spec, ext_spec = specs(row_count, None)
    first = carry is None
    if first:
        operands = [slots, counts, queries, keys, values]
        in_specs = [tile_spec, ext_spec, ext_spec]
        out_types = [jnp.float32] * 3
    else:
        operands = [slots, counts, queries, *keys, *values, *carry]
        in_specs = [tile_spec] + [ext_spec] * 6 + [tile_spec] * 3
        out_types = [jnp.bfloat16, jnp.float32]
    return pl.pallas_call(
        make_forward_kernel(first),
        grid_spec=pltpu.PrefetchScalarGridSpec(
            num_scalar_prefetch=2,
            grid=(col_count // HD, row_count // TILE),
            in_specs=in_specs,
            out_specs=[tile_spec] * len(out_types),
            scratch_shapes=[pltpu.VMEM((KSLOT, TILE, TILE), jnp.float32)],
        ),
        out_shape=[jax.ShapeDtypeStruct((row_count, col_count), t) for t in out_types],
        compiler_params=pltpu.CompilerParams(
            dimension_semantics=("arbitrary", "arbitrary"),
            vmem_limit_bytes=48 * 1024 * 1024,
        ),
    )(*operands)


def attention_backward(slots, counts, queries, grads, out, lse, keys, values, dq_in=None):
    row_count, col_count = queries.shape
    ext_rows = 3 * row_count
    own = dq_in is not None
    acc_rows = row_count if own else ext_rows - row_count
    tile_spec, ext_spec = specs(row_count, ext_rows)
    acc_spec = pl.BlockSpec((acc_rows, HD), lambda h, a, sl, ct: (0, h))
    operands = [slots, counts, queries, grads, out, lse, *keys, *values]
    in_specs = [tile_spec] * 4 + [ext_spec] * 6
    if own:
        operands.append(dq_in)
        in_specs.append(tile_spec)
    if own:
        out_specs = [tile_spec, acc_spec, acc_spec]
        out_shape = [
            jax.ShapeDtypeStruct((row_count, col_count), jnp.bfloat16),
            jax.ShapeDtypeStruct((acc_rows, col_count), jnp.float32),
            jax.ShapeDtypeStruct((acc_rows, col_count), jnp.float32),
        ]
        scratch = []
    else:
        rim_spec = pl.BlockSpec((2, row_count, HD), lambda h, a, sl, ct: (0, 0, h))
        out_specs = [tile_spec, rim_spec, rim_spec]
        out_shape = [
            jax.ShapeDtypeStruct((row_count, col_count), jnp.float32),
            jax.ShapeDtypeStruct((2, row_count, col_count), jnp.bfloat16),
            jax.ShapeDtypeStruct((2, row_count, col_count), jnp.bfloat16),
        ]
        scratch = [pltpu.VMEM((acc_rows, HD), jnp.float32)] * 2
    return pl.pallas_call(
        make_backward_kernel(own),
        grid_spec=pltpu.PrefetchScalarGridSpec(
            num_scalar_prefetch=2,
            grid=(col_count // HD, row_count // TILE),
            in_specs=in_specs,
            out_specs=out_specs,
            scratch_shapes=scratch,
        ),
        out_shape=out_shape,
        compiler_params=pltpu.CompilerParams(
            dimension_semantics=("arbitrary", "arbitrary"),
            vmem_limit_bytes=48 * 1024 * 1024,
        ),
    )(*operands)


def split_slots(listed, base_tile, first_tile, own_tiles):
    allowed = listed >= 0
    mine = allowed & (listed >= first_tile) & (listed < first_tile + own_tiles)
    near = allowed & ~mine
    slots = jnp.where(allowed, listed - base_tile, 0)
    lists = []
    places = jnp.arange(listed.shape[1], dtype=jnp.int32)
    for keep in (mine, near):
        place = jnp.sum(
            keep[:, :, None] & (places[:, None] <= places[None, :])[None], axis=1
        ).astype(jnp.int32) - 1
        hit = keep[:, :, None] & (place[:, :, None] == places[None, None, :])
        picked = jnp.sum(jnp.where(hit, slots[:, :, None], 0), axis=1)
        lists.append((picked.reshape(-1).astype(jnp.int32), jnp.sum(keep.astype(jnp.int32), axis=1)))
    return lists


def shards(queries, key_states, value_states, out_grads, pattern):
    row_count, col_count = queries.shape
    own_tiles = row_count // TILE
    first_tile = lax.axis_index("ctx") * own_tiles
    base_tile = first_tile - SPT
    keys = with_halo(key_states, "ctx")
    values = with_halo(value_states, "ctx")
    grads_heads = lax.all_to_all(out_grads, "head", split_axis=1, concat_axis=0, tiled=True)
    listed = lax.dynamic_slice_in_dim(pattern, first_tile, own_tiles, 0)
    (own_slots, own_counts), (near_slots, near_counts) = split_slots(
        listed, base_tile, first_tile, own_tiles
    )
    carry = attention_forward(own_slots, own_counts, queries, key_states, value_states)
    out, lse = attention_forward(
        near_slots, near_counts, queries, keys, values, carry
    )
    attended = lax.all_to_all(out, "head", split_axis=0, concat_axis=1, tiled=True)
    dq_part, lower_part, upper_part = attention_backward(
        near_slots, near_counts, queries, grads_heads, out, lse, keys, values
    )
    dq, dk_own, dv_own = attention_backward(
        own_slots, own_counts, queries, grads_heads, out, lse, keys, values, dq_part
    )
    own_part = jnp.stack((dk_own, dv_own))
    from_above = from_behind(lower_part, "ctx", -1).astype(jnp.float32)
    from_below = from_behind(upper_part, "ctx", 1).astype(jnp.float32)
    total = own_part + from_above + from_below
    key_grads = (total[0] * SCALE).astype(jnp.bfloat16)
    value_grads = total[1].astype(jnp.bfloat16)
    return (attended, dq, key_grads, value_grads)


def solution(mesh):
    return jax.shard_map(
        shards,
        mesh=mesh,
        in_specs=(
            P("ctx", "head"),
            P("ctx", "head"),
            P("ctx", "head"),
            P(("ctx", "head"), None),
            P(),
        ),
        out_specs=(P(("ctx", "head"), None), P("ctx", "head"), P("ctx", "head"), P("ctx", "head")),
        check_vma=False,
    )
```
